256 devices in a mesh: runs: 32 (over y, x, core), cells: 8 (over z).
Axes of the slice: x: 4, y: 4, z: 8, core: 2. Of those that a mesh axis runs over, the one named last changes fastest.
Arguments:
- train_depth: bfloat16 [16384, 32768], P('runs', 'cells'), may hold values from -6 to 6
- train_basis: bfloat16 [16384, 512], P('runs', 'cells'), may hold values from -6 to 6
- sample_basis: bfloat16 [16384, 512], P('runs', 'cells'), may hold values from -0.25 to 0.25
- gram_inverse: float32 [512, 512], replicated, may hold values from -8 to 8
Outputs:
- peak_depth: bfloat16 [16384, 32768], P('runs', 'cells')
The draws below stay inside these ranges and needn't reach their ends.
All inputs are finite; a program needn't handle non-finite values.
Results may differ from the reference program's by a relative error of at most 0.0049.
Values may be sent and summed in bfloat16 or wider, within the bound.
No kernel may reach another device: no remote copies, remote signals or barrier semaphores. Data moves between devices by JAX's collectives and lax.ppermute only.
A program may use at most 64 MiB of HBM per device.

```python
import math
import jax
import jax.numpy as jnp
from jax import lax

TERMS = 512
CELLS = 32768
TRAIN_RUNS = 16384
SAMPLES = 16384


def draw_gram_inverse(key, part):
    k_diag, k_off = jax.random.split(key, 2)
    diag_vals = jnp.exp(jax.random.uniform(k_diag, (TERMS,), jnp.float32, math.log(0.5), math.log(2.0)))
    off_vals = jnp.clip(jax.random.normal(k_off, (TERMS, TERMS), jnp.float32), -4.0, 4.0) * (0.4 / math.sqrt(TERMS))
    ident = (jnp.arange(TERMS)[:, None] == jnp.arange(TERMS)[None, :]).astype(jnp.float32)
    result = ident * diag_vals[None, :] + (1.0 - ident) * off_vals
    return result


def level_of(stream_key, dims, pieces, least, largest):
    level = 1.0
    for axis_at, blocks in pieces:
        heights = jax.random.uniform(jax.random.fold_in(jax.random.fold_in(stream_key, 6), axis_at), (blocks,), jnp.float32, least / len(pieces), largest / len(pieces))
        level = level * jnp.repeat(jnp.exp(heights), dims[axis_at] // blocks).reshape((-1,) + (1,) * (len(dims) - 1 - axis_at))
    return level


def centred(stream_key, dims, width, reach, cuts=(), held_as=jnp.bfloat16):
    values = jax.random.normal(stream_key, dims, jnp.float32) * width
    if len(cuts) > 0:
        values = level_of(stream_key, dims, cuts, -0.22, 0.18) * values
    return jnp.clip(values, min=-reach, max=reach).astype(held_as)


def setup_inputs(seed: int = 0) -> dict:
    arg_keys = jax.random.split(jax.random.key(seed), 5)
    train_depth = centred(arg_keys[0], (TRAIN_RUNS, CELLS), 1.0, 6.0, ((0, 32), (1, 8)))
    train_basis = centred(arg_keys[1], (TRAIN_RUNS, TERMS), 1.0, 6.0, ((0, 32), (1, 8)))
    sample_basis = centred(arg_keys[2], (SAMPLES, TERMS), TERMS ** -0.5, 0.25, ((0, 32), (1, 8)))
    gram_inverse = draw_gram_inverse(jax.random.fold_in(arg_keys[4], 71), 0)
    return {"train_depth": train_depth, "train_basis": train_basis, "sample_basis": sample_basis, "gram_inverse": gram_inverse}


def reference(train_depth, train_basis, sample_basis, gram_inverse):
    moments = lax.dot_general(train_basis, train_depth, (((0,), (0,)), ((), ())), preferred_element_type=jnp.float32)
    moments = moments * (1.0 / math.sqrt(TRAIN_RUNS))
    coeffs = jnp.dot(gram_inverse, moments, precision=lax.Precision.HIGHEST).astype(jnp.bfloat16)
    return jnp.dot(sample_basis, coeffs, preferred_element_type=jnp.float32).astype(jnp.bfloat16)
```

```python
import math

import jax
import jax.numpy as jnp
from jax import lax
from jax.sharding import PartitionSpec as P


def per_device(train_depth, train_basis, sample_basis, gram_inverse):
    terms_here = train_basis.shape[1]
    n_cells = lax.axis_size("cells")
    total_runs = train_depth.shape[0] * lax.axis_size("runs")
    norm_scale = 1.0 / math.sqrt(total_runs)
    both = jnp.concatenate([train_basis, sample_basis], axis=1).T
    both_full = lax.all_gather(both, "cells", axis=0, tiled=False)
    train_t = both_full[:, :terms_here, :].reshape(n_cells * terms_here, -1)
    sample_t = both_full[:, terms_here:, :].reshape(n_cells * terms_here, -1)
    partial_t = lax.dot_general(
        train_depth, train_t, (((0,), (1,)), ((), ())), preferred_element_type=jnp.float32
    )
    moments_t = lax.psum_scatter(partial_t, "runs", scatter_dimension=0, tiled=True) * norm_scale
    coeffs_t = lax.dot_general(
        moments_t, gram_inverse, (((1,), (1,)), ((), ())), precision=lax.Precision.HIGHEST
    ).astype(jnp.bfloat16)
    coeffs_full_t = lax.all_gather(coeffs_t, "runs", axis=0, tiled=True)
    peak_depth = lax.dot_general(
        sample_t, coeffs_full_t, (((0,), (1,)), ((), ())), preferred_element_type=jnp.float32
    ).astype(jnp.bfloat16)
    return peak_depth


def solution(mesh):
    in_specs = (P("runs", "cells"), P("runs", "cells"), P("runs", "cells"), P())
    out_specs = P("runs", "cells")
    return jax.shard_map(
        per_device, mesh=mesh, in_specs=in_specs, out_specs=out_specs, check_vma=False
    )
```

```python
import math

import jax
import jax.numpy as jnp
from jax import lax
from jax.sharding import PartitionSpec as P


def per_device(train_depth, train_basis, sample_basis, gram_inverse):
    terms_here = train_basis.shape[1]
    runs_here = train_basis.shape[0]
    n_cells = lax.axis_size("cells")
    total_runs = train_depth.shape[0] * lax.axis_size("runs")
    norm_scale = 1.0 / math.sqrt(total_runs)
    both = jnp.concatenate([train_basis, sample_basis], axis=1)
    both_full = lax.all_gather(both, "cells", axis=1, tiled=False)
    train_full = both_full[:, :, :terms_here].reshape(runs_here, n_cells * terms_here)
    sample_full = both_full[:, :, terms_here:].reshape(runs_here, n_cells * terms_here)
    folded = lax.dot_general(
        train_full.astype(jnp.float32), gram_inverse, (((1,), (1,)), ((), ())),
        precision=lax.Precision.HIGHEST,
    )
    folded_hi = folded.astype(jnp.bfloat16)
    folded_lo = (folded - folded_hi.astype(jnp.float32)).astype(jnp.bfloat16)
    dims = (((0,), (0,)), ((), ()))
    partial_t = lax.dot_general(
        train_depth, folded_hi, dims, preferred_element_type=jnp.float32
    ) + lax.dot_general(train_depth, folded_lo, dims, preferred_element_type=jnp.float32)
    coeffs_t = (lax.psum(partial_t, "runs") * norm_scale).astype(jnp.bfloat16)
    peak_depth = lax.dot_general(
        sample_full, coeffs_t, (((1,), (1,)), ((), ())), preferred_element_type=jnp.float32
    ).astype(jnp.bfloat16)
    return peak_depth


def solution(mesh):
    in_specs = (P("runs", "cells"), P("runs", "cells"), P("runs", "cells"), P())
    out_specs = P("runs", "cells")
    return jax.shard_map(
        per_device, mesh=mesh, in_specs=in_specs, out_specs=out_specs, check_vma=False
    )
```

```python
import math

import jax
import jax.numpy as jnp
from jax import lax
from jax.sharding import PartitionSpec as P


def _factor_runs(n_runs):
    nc = 2 if n_runs % 2 == 0 else 1
    rest = n_runs // nc
    nx = int(math.isqrt(rest))
    while rest % nx:
        nx -= 1
    return rest // nx, nx, nc


def _perm(n, fn):
    return [(i, fn(i)) for i in range(n)]


def _ring_reduce_scatter(v, axis, n, pos, fwd, bwd):
    if n == 1:
        return v
    m, h = v.shape[0] // n, v.shape[1] // 2
    lo, hi = v[:, :h], v[:, h:]

    def piece(src, idx):
        return lax.dynamic_slice_in_dim(src, lax.rem(idx + 2 * n, n) * m, m, axis=0)

    acc_f, acc_b = piece(lo, pos - 1), piece(hi, pos + 1)
    for s in range(n - 1):
        acc_f = lax.ppermute(acc_f, axis, fwd) + piece(lo, pos - s - 2)
        acc_b = lax.ppermute(acc_b, axis, bwd) + piece(hi, pos + s + 2)
    return jnp.concatenate([acc_f, acc_b], axis=1)


def _ring_all_gather(c, axis, n, pos, fwd, bwd):
    if n == 1:
        return c
    m, k = c.shape
    h = k // 2
    out = jnp.zeros((n * m, k), c.dtype)
    out = lax.dynamic_update_slice(out, c, (pos * m, 0))
    cur_f, cur_b = c[:, :h], c[:, h:]
    for s in range(n - 1):
        cur_f = lax.ppermute(cur_f, axis, fwd)
        cur_b = lax.ppermute(cur_b, axis, bwd)
        out = lax.dynamic_update_slice(out, cur_f, (lax.rem(pos - s - 1 + n, n) * m, 0))
        out = lax.dynamic_update_slice(out, cur_b, (lax.rem(pos + s + 1, n) * m, h))
    return out


def _gather_cells(blk, n):
    q = lax.axis_index("cells")
    rows, w = blk.shape
    out = jnp.zeros((rows, n, w), blk.dtype)
    out = lax.dynamic_update_slice(out, blk[:, None, :], (0, q, 0))
    fwd = _perm(n, lambda i: (i + 1) % n)
    bwd = _perm(n, lambda i: (i - 1) % n)
    n_f = n // 2
    n_b = n - 1 - n_f
    cur_f = cur_b = blk
    for s in range(max(n_f, n_b)):
        if s < n_f:
            cur_f = lax.ppermute(cur_f, "cells", fwd)
            out = lax.dynamic_update_slice(out, cur_f[:, None, :], (0, lax.rem(q - s - 1 + n, n), 0))
        if s < n_b:
            cur_b = lax.ppermute(cur_b, "cells", bwd)
            out = lax.dynamic_update_slice(out, cur_b[:, None, :], (0, lax.rem(q + s + 1, n), 0))
    return out


def per_device(train_depth, train_basis, sample_basis, gram_inverse):
    runs_here, terms_here = train_basis.shape
    n_cells = lax.axis_size("cells")
    n_runs = lax.axis_size("runs")
    total_runs = train_depth.shape[0] * n_runs
    norm_scale = 1.0 / math.sqrt(total_runs)

    both = jnp.concatenate([train_basis, sample_basis], axis=1)
    both_full = _gather_cells(both, n_cells)
    train_full = both_full[:, :, :terms_here].reshape(runs_here, n_cells * terms_here)
    sample_full = both_full[:, :, terms_here:].reshape(runs_here, n_cells * terms_here)

    folded = lax.dot_general(
        train_full.astype(jnp.float32), gram_inverse, (((1,), (1,)), ((), ())),
        precision=lax.Precision.HIGHEST,
    )
    folded_hi = lax.reduce_precision(folded, exponent_bits=8, mantissa_bits=7)
    folded_lo = (folded - folded_hi).astype(jnp.bfloat16)
    folded_hi = folded_hi.astype(jnp.bfloat16)
    dims = (((0,), (0,)), ((), ()))
    partial_t = lax.dot_general(
        train_depth, folded_hi, dims, preferred_element_type=jnp.float32
    ) + lax.dot_general(train_depth, folded_lo, dims, preferred_element_type=jnp.float32)

    ny, nx, nc = _factor_runs(n_runs)
    r = lax.axis_index("runs")
    core = lax.rem(r, nc)
    xi = lax.rem(r // nc, nx)
    yi = r // (nc * nx)

    def shift_x(d):
        return lambda i: ((i // (nc * nx)) * nx + (i // nc % nx + d) % nx) * nc + i % nc

    def shift_y(d):
        return lambda i: (((i // (nc * nx)) + d) % ny * nx + i // nc % nx) * nc + i % nc

    xf, xb = _perm(n_runs, shift_x(1)), _perm(n_runs, shift_x(-1))
    yf, yb = _perm(n_runs, shift_y(1)), _perm(n_runs, shift_y(-1))

    cells_here = partial_t.shape[0]
    if nc > 1:
        core_perm = _perm(n_runs, lambda i: i - i % nc + (i % nc + 1) % nc)
        half = cells_here // nc
        mine = lax.dynamic_slice_in_dim(partial_t, core * half, half, axis=0)
        other = lax.dynamic_slice_in_dim(partial_t, (1 - core) * half, half, axis=0)
        summed = lax.ppermute(other, "runs", core_perm) + mine
    else:
        summed = partial_t
    k2 = summed.shape[1] // 2
    part_a = _ring_reduce_scatter(summed[:, :k2], "runs", nx, xi, xf, xb)
    part_a = _ring_reduce_scatter(part_a, "runs", ny, yi, yf, yb)
    part_b = _ring_reduce_scatter(summed[:, k2:], "runs", ny, yi, yf, yb)
    part_b = _ring_reduce_scatter(part_b, "runs", nx, xi, xf, xb)
    coeff_a = (part_a * norm_scale).astype(jnp.bfloat16)
    coeff_b = (part_b * norm_scale).astype(jnp.bfloat16)
    coeff_a = _ring_all_gather(coeff_a, "runs", ny, yi, yf, yb)
    coeff_a = _ring_all_gather(coeff_a, "runs", nx, xi, xf, xb)
    coeff_b = _ring_all_gather(coeff_b, "runs", nx, xi, xf, xb)
    coeff_b = _ring_all_gather(coeff_b, "runs", ny, yi, yf, yb)
    coeffs_t = jnp.concatenate([coeff_a, coeff_b], axis=1)
    if nc > 1:
        theirs = lax.ppermute(coeffs_t, "runs", core_perm)
        full = jnp.zeros((cells_here,) + coeffs_t.shape[1:], coeffs_t.dtype)
        full = lax.dynamic_update_slice_in_dim(full, coeffs_t, core * half, axis=0)
        coeffs_t = lax.dynamic_update_slice_in_dim(full, theirs, (1 - core) * half, axis=0)

    peak_depth = lax.dot_general(
        sample_full, coeffs_t, (((1,), (1,)), ((), ())), preferred_element_type=jnp.float32
    ).astype(jnp.bfloat16)
    return peak_depth


def solution(mesh):
    in_specs = (P("runs", "cells"), P("runs", "cells"), P("runs", "cells"), P())
    out_specs = P("runs", "cells")
    return jax.shard_map(
        per_device, mesh=mesh, in_specs=in_specs, out_specs=out_specs, check_vma=False
    )
```

```python
import math

import jax
import jax.numpy as jnp
from jax import lax
from jax.sharding import PartitionSpec as P


def _factor_runs(n_runs):
    nc = 2 if n_runs % 2 == 0 else 1
    rest = n_runs // nc
    nx = int(math.isqrt(rest))
    while rest % nx:
        nx -= 1
    return rest // nx, nx, nc


def _perm(n, fn):
    return [(i, fn(i)) for i in range(n)]


def _ring_reduce_scatter(v, chunk_axis, axis, n, pos, fwd, bwd):
    if n == 1:
        return lax.index_in_dim(v, 0, chunk_axis, keepdims=False)
    h = v.shape[-1] // 2
    lo, hi = v[..., :h], v[..., h:]

    def piece(src, idx):
        return lax.dynamic_index_in_dim(src, lax.rem(idx + 2 * n, n), chunk_axis, keepdims=False)

    acc_f, acc_b = piece(lo, pos - 1), piece(hi, pos + 1)
    for s in range(n - 1):
        acc_f = lax.ppermute(acc_f, axis, fwd) + piece(lo, pos - s - 2)
        acc_b = lax.ppermute(acc_b, axis, bwd) + piece(hi, pos + s + 2)
    return jnp.concatenate([acc_f, acc_b], axis=-1)


def _ring_all_gather(c, axis, n, pos, fwd, bwd):
    if n == 1:
        return c[None]
    h = c.shape[-1] // 2
    out = jnp.zeros((n,) + c.shape, c.dtype)
    zeros = (0,) * c.ndim
    out = lax.dynamic_update_slice(out, c[None], (pos,) + zeros)
    cur_f, cur_b = c[..., :h], c[..., h:]
    half_at = zeros[:-1] + (h,)
    for s in range(n - 1):
        cur_f = lax.ppermute(cur_f, axis, fwd)
        cur_b = lax.ppermute(cur_b, axis, bwd)
        out = lax.dynamic_update_slice(out, cur_f[None], (lax.rem(pos - s - 1 + n, n),) + zeros)
        out = lax.dynamic_update_slice(out, cur_b[None], (lax.rem(pos + s + 1, n),) + half_at)
    return out


def _gather_cells(blk, n):
    q = lax.axis_index("cells")
    rows, w = blk.shape
    out = jnp.zeros((rows, n, w), blk.dtype)
    out = lax.dynamic_update_slice(out, blk[:, None, :], (0, q, 0))
    fwd = _perm(n, lambda i: (i + 1) % n)
    bwd = _perm(n, lambda i: (i - 1) % n)
    n_f = n // 2
    n_b = n - 1 - n_f
    cur_f = cur_b = blk
    for s in range(max(n_f, n_b)):
        if s < n_f:
            cur_f = lax.ppermute(cur_f, "cells", fwd)
            out = lax.dynamic_update_slice(out, cur_f[:, None, :], (0, lax.rem(q - s - 1 + n, n), 0))
        if s < n_b:
            cur_b = lax.ppermute(cur_b, "cells", bwd)
            out = lax.dynamic_update_slice(out, cur_b[:, None, :], (0, lax.rem(q + s + 1, n), 0))
    return out


def per_device(train_depth, train_basis, sample_basis, gram_inverse):
    runs_here, terms_here = train_basis.shape
    n_cells = lax.axis_size("cells")
    n_runs = lax.axis_size("runs")
    total_runs = train_depth.shape[0] * n_runs
    norm_scale = 1.0 / math.sqrt(total_runs)

    train_full = _gather_cells(train_basis, n_cells).reshape(runs_here, n_cells * terms_here)
    sample_t = lax.all_gather(sample_basis.T, "cells", axis=0, tiled=True)

    folded = lax.dot_general(
        train_full.astype(jnp.float32), gram_inverse, (((1,), (1,)), ((), ())),
        precision=lax.Precision.HIGHEST,
    )
    folded_hi = lax.reduce_precision(folded, exponent_bits=8, mantissa_bits=7)
    folded_lo = (folded - folded_hi).astype(jnp.bfloat16)
    folded_hi = folded_hi.astype(jnp.bfloat16)
    dims = (((0,), (0,)), ((), ()))
    partial_t = lax.dot_general(
        train_depth, folded_hi, dims, preferred_element_type=jnp.float32
    ) + lax.dot_general(train_depth, folded_lo, dims, preferred_element_type=jnp.float32)

    ny, nx, nc = _factor_runs(n_runs)
    r = lax.axis_index("runs")
    core = lax.rem(r, nc)
    xi = lax.rem(r // nc, nx)
    yi = r // (nc * nx)

    def shift_x(d):
        return lambda i: ((i // (nc * nx)) * nx + (i // nc % nx + d) % nx) * nc + i % nc

    def shift_y(d):
        return lambda i: (((i // (nc * nx)) + d) % ny * nx + i // nc % nx) * nc + i % nc

    xf, xb = _perm(n_runs, shift_x(1)), _perm(n_runs, shift_x(-1))
    yf, yb = _perm(n_runs, shift_y(1)), _perm(n_runs, shift_y(-1))

    cells_here, n_terms = partial_t.shape
    half = cells_here // nc
    if nc > 1:
        core_perm = _perm(n_runs, lambda i: i - i % nc + (i % nc + 1) % nc)
        mine = lax.dynamic_slice_in_dim(partial_t, core * half, half, axis=0)
        other = lax.dynamic_slice_in_dim(partial_t, (1 - core) * half, half, axis=0)
        summed = lax.ppermute(other, "runs", core_perm) + mine
    else:
        summed = partial_t
    m = half // (nx * ny)
    view = summed.reshape(nx, ny, m, n_terms)
    k2 = n_terms // 2
    part_a = _ring_reduce_scatter(view[..., :k2], 0, "runs", nx, xi, xf, xb)
    part_a = _ring_reduce_scatter(part_a, 0, "runs", ny, yi, yf, yb)
    part_b = _ring_reduce_scatter(view[..., k2:], 1, "runs", ny, yi, yf, yb)
    part_b = _ring_reduce_scatter(part_b, 0, "runs", nx, xi, xf, xb)
    coeffs = (jnp.concatenate([part_a, part_b], axis=-1) * norm_scale).astype(jnp.bfloat16)
    coeffs = _ring_all_gather(coeffs, "runs", ny, yi, yf, yb)
    coeffs = _ring_all_gather(coeffs, "runs", nx, xi, xf, xb)
    coeffs_t = coeffs.reshape(half, n_terms)
    if nc > 1:
        theirs = lax.ppermute(coeffs_t, "runs", core_perm)
        full = jnp.zeros((cells_here, n_terms), coeffs_t.dtype)
        full = lax.dynamic_update_slice_in_dim(full, coeffs_t, core * half, axis=0)
        coeffs_t = lax.dynamic_update_slice_in_dim(full, theirs, (1 - core) * half, axis=0)

    peak_depth = lax.dot_general(
        sample_t, coeffs_t, (((0,), (1,)), ((), ())), preferred_element_type=jnp.float32
    ).astype(jnp.bfloat16)
    return peak_depth


def solution(mesh):
    in_specs = (P("runs", "cells"), P("runs", "cells"), P("runs", "cells"), P())
    out_specs = P("runs", "cells")
    return jax.shard_map(
        per_device, mesh=mesh, in_specs=in_specs, out_specs=out_specs, check_vma=False
    )
```

```python
import math

import jax
import jax.numpy as jnp
from jax import lax
from jax.sharding import PartitionSpec as P


def _factor_runs(n_runs):
    nc = 2 if n_runs % 2 == 0 else 1
    rest = n_runs // nc
    nx = int(math.isqrt(rest))
    while rest % nx:
        nx -= 1
    return rest // nx, nx, nc


def _perm(n, fn):
    return [(i, fn(i)) for i in range(n)]


def _ring_reduce_scatter(v, axis, n, pos, fwd, bwd):
    if n == 1:
        return v
    m = v.shape[0] // n
    if bwd is None:
        acc = lax.dynamic_slice_in_dim(v, lax.rem(pos - 1 + n, n) * m, m, axis=0)
        for s in range(n - 1):
            acc = lax.ppermute(acc, axis, fwd) + lax.dynamic_slice_in_dim(
                v, lax.rem(pos - s - 2 + 2 * n, n) * m, m, axis=0
            )
        return acc
    h = v.shape[1] // 2
    lo, hi = v[:, :h], v[:, h:]

    def piece(src, idx):
        return lax.dynamic_slice_in_dim(src, lax.rem(idx + 2 * n, n) * m, m, axis=0)

    acc_f, acc_b = piece(lo, pos - 1), piece(hi, pos + 1)
    for s in range(n - 1):
        acc_f = lax.ppermute(acc_f, axis, fwd) + piece(lo, pos - s - 2)
        acc_b = lax.ppermute(acc_b, axis, bwd) + piece(hi, pos + s + 2)
    return jnp.concatenate([acc_f, acc_b], axis=1)


def _ring_all_gather(c, axis, n, pos, fwd, bwd):
    if n == 1:
        return c
    m, k = c.shape
    h = k // 2
    out = jnp.zeros((n * m, k), c.dtype)
    out = lax.dynamic_update_slice(out, c, (pos * m, 0))
    if bwd is None:
        cur = c
        for s in range(n - 1):
            cur = lax.ppermute(cur, axis, fwd)
            out = lax.dynamic_update_slice(out, cur, (lax.rem(pos - s - 1 + n, n) * m, 0))
        return out
    cur_f, cur_b = c[:, :h], c[:, h:]
    for s in range(n - 1):
        cur_f = lax.ppermute(cur_f, axis, fwd)
        cur_b = lax.ppermute(cur_b, axis, bwd)
        out = lax.dynamic_update_slice(out, cur_f, (lax.rem(pos - s - 1 + n, n) * m, 0))
        out = lax.dynamic_update_slice(out, cur_b, (lax.rem(pos + s + 1, n) * m, h))
    return out


def _gather_cells(blk, n):
    q = lax.axis_index("cells")
    rows, w = blk.shape
    out = jnp.zeros((rows, n, w), blk.dtype)
    out = lax.dynamic_update_slice(out, blk[:, None, :], (0, q, 0))
    fwd = _perm(n, lambda i: (i + 1) % n)
    bwd = _perm(n, lambda i: (i - 1) % n)
    n_f = n // 2
    n_b = n - 1 - n_f
    cur_f = cur_b = blk
    for s in range(max(n_f, n_b)):
        if s < n_f:
            cur_f = lax.ppermute(cur_f, "cells", fwd)
            out = lax.dynamic_update_slice(out, cur_f[:, None, :], (0, lax.rem(q - s - 1 + n, n), 0))
        if s < n_b:
            cur_b = lax.ppermute(cur_b, "cells", bwd)
            out = lax.dynamic_update_slice(out, cur_b[:, None, :], (0, lax.rem(q + s + 1, n), 0))
    return out


def per_device(train_depth, train_basis, sample_basis, gram_inverse):
    runs_here, terms_here = train_basis.shape
    n_cells = lax.axis_size("cells")
    n_runs = lax.axis_size("runs")
    total_runs = train_depth.shape[0] * n_runs
    norm_scale = 1.0 / math.sqrt(total_runs)

    both = jnp.concatenate([train_basis, sample_basis], axis=1)
    both_full = _gather_cells(both, n_cells)
    train_full = both_full[:, :, :terms_here].reshape(runs_here, n_cells * terms_here)
    sample_full = both_full[:, :, terms_here:].reshape(runs_here, n_cells * terms_here)

    folded = lax.dot_general(
        train_full.astype(jnp.float32), gram_inverse, (((1,), (1,)), ((), ())),
        precision=lax.Precision.HIGHEST,
    )
    folded_hi = lax.reduce_precision(folded, exponent_bits=8, mantissa_bits=7)
    folded_lo = (folded - folded_hi).astype(jnp.bfloat16)
    folded_hi = folded_hi.astype(jnp.bfloat16)
    dims = (((0,), (0,)), ((), ()))

    def project(depth):
        return lax.dot_general(
            depth, folded_hi, dims, preferred_element_type=jnp.float32
        ) + lax.dot_general(depth, folded_lo, dims, preferred_element_type=jnp.float32)

    ny, nx, nc = _factor_runs(n_runs)
    r = lax.axis_index("runs")
    core = lax.rem(r, nc)
    xi = lax.rem(r // nc, nx)
    yi = r // (nc * nx)

    def shift_x(d):
        return lambda i: ((i // (nc * nx)) * nx + (i // nc % nx + d) % nx) * nc + i % nc

    def shift_y(d):
        return lambda i: (((i // (nc * nx)) + d) % ny * nx + i // nc % nx) * nc + i % nc

    xf, xb = _perm(n_runs, shift_x(1)), _perm(n_runs, shift_x(-1))
    yf, yb = _perm(n_runs, shift_y(1)), _perm(n_runs, shift_y(-1))

    cells_here = train_depth.shape[1]
    if nc > 1:
        core_perm = _perm(n_runs, lambda i: i - i % nc + (i % nc + 1) % nc)
        half = cells_here // nc
        other = project(lax.dynamic_slice_in_dim(train_depth, (1 - core) * half, half, axis=1))
        received = lax.ppermute(other, "runs", core_perm)
        mine = project(lax.dynamic_slice_in_dim(train_depth, core * half, half, axis=1))
        summed = received + mine
    else:
        summed = project(train_depth)
    k2 = summed.shape[1] // 2
    part_a = _ring_reduce_scatter(summed[:, :k2], "runs", nx, xi, xf, xb)
    part_a = _ring_reduce_scatter(part_a, "runs", ny, yi, yf, None)
    part_b = _ring_reduce_scatter(summed[:, k2:], "runs", ny, yi, yf, yb)
    part_b = _ring_reduce_scatter(part_b, "runs", nx, xi, xf, None)
    coeff_a = (part_a * norm_scale).astype(jnp.bfloat16)
    coeff_b = (part_b * norm_scale).astype(jnp.bfloat16)
    coeff_a = _ring_all_gather(coeff_a, "runs", ny, yi, yf, None)
    coeff_a = _ring_all_gather(coeff_a, "runs", nx, xi, xf, xb)
    coeff_b = _ring_all_gather(coeff_b, "runs", nx, xi, xf, None)
    coeff_b = _ring_all_gather(coeff_b, "runs", ny, yi, yf, yb)
    coeffs_t = jnp.concatenate([coeff_a, coeff_b], axis=1)

    def surrogate(coeffs):
        return lax.dot_general(
            sample_full, coeffs, (((1,), (1,)), ((), ())), preferred_element_type=jnp.float32
        ).astype(jnp.bfloat16)

    if nc == 1:
        return surrogate(coeffs_t)
    theirs = lax.ppermute(coeffs_t, "runs", core_perm)
    peak_depth = jnp.zeros((sample_full.shape[0], cells_here), jnp.bfloat16)
    peak_depth = lax.dynamic_update_slice_in_dim(peak_depth, surrogate(coeffs_t), core * half, axis=1)
    return lax.dynamic_update_slice_in_dim(peak_depth, surrogate(theirs), (1 - core) * half, axis=1)


def solution(mesh):
    in_specs = (P("runs", "cells"), P("runs", "cells"), P("runs", "cells"), P())
    out_specs = P("runs", "cells")
    return jax.shard_map(
        per_device, mesh=mesh, in_specs=in_specs, out_specs=out_specs, check_vma=False
    )
```

```python
import math

import jax
import jax.numpy as jnp
from jax import lax
from jax.sharding import PartitionSpec as P


def _factor_runs(n_runs):
    nc = 2 if n_runs % 2 == 0 else 1
    rest = n_runs // nc
    nx = int(math.isqrt(rest))
    while rest % nx:
        nx -= 1
    return rest // nx, nx, nc


def _perm(n, fn):
    return [(i, fn(i)) for i in range(n)]


def _ring_reduce_scatter(v, axis, n, pos, fwd, bwd):
    if n == 1:
        return v
    m = v.shape[0] // n
    if bwd is None:
        acc = lax.dynamic_slice_in_dim(v, lax.rem(pos - 1 + n, n) * m, m, axis=0)
        for s in range(n - 1):
            acc = lax.ppermute(acc, axis, fwd) + lax.dynamic_slice_in_dim(
                v, lax.rem(pos - s - 2 + 2 * n, n) * m, m, axis=0
            )
        return acc
    h = v.shape[1] // 2
    lo, hi = v[:, :h], v[:, h:]

    def piece(src, idx):
        return lax.dynamic_slice_in_dim(src, lax.rem(idx + 2 * n, n) * m, m, axis=0)

    acc_f, acc_b = piece(lo, pos - 1), piece(hi, pos + 1)
    for s in range(n - 1):
        acc_f = lax.ppermute(acc_f, axis, fwd) + piece(lo, pos - s - 2)
        acc_b = lax.ppermute(acc_b, axis, bwd) + piece(hi, pos + s + 2)
    return jnp.concatenate([acc_f, acc_b], axis=1)


def _ring_all_gather(c, axis, n, pos, fwd, bwd):
    if n == 1:
        return c
    m, k = c.shape
    h = k // 2
    out = jnp.zeros((n * m, k), c.dtype)
    out = lax.dynamic_update_slice(out, c, (pos * m, 0))
    if bwd is None:
        cur = c
        for s in range(n - 1):
            cur = lax.ppermute(cur, axis, fwd)
            out = lax.dynamic_update_slice(out, cur, (lax.rem(pos - s - 1 + n, n) * m, 0))
        return out
    cur_f, cur_b = c[:, :h], c[:, h:]
    for s in range(n - 1):
        cur_f = lax.ppermute(cur_f, axis, fwd)
        cur_b = lax.ppermute(cur_b, axis, bwd)
        out = lax.dynamic_update_slice(out, cur_f, (lax.rem(pos - s - 1 + n, n) * m, 0))
        out = lax.dynamic_update_slice(out, cur_b, (lax.rem(pos + s + 1, n) * m, h))
    return out


def _reduce_scatter4(v, axis, pos, fwd, bwd):
    m, k = v.shape[0] // 4, v.shape[1]
    h = k // 2

    def chunk(j):
        return lax.dynamic_slice_in_dim(v, lax.rem(pos + j + 4, 4) * m, m, axis=0)

    far = chunk(2)
    got_f = lax.ppermute(jnp.concatenate([chunk(1), far[:, :h]], axis=1), axis, fwd)
    got_b = lax.ppermute(jnp.concatenate([chunk(-1), far[:, h:]], axis=1), axis, bwd)
    far_f = lax.ppermute(got_f[:, k:], axis, fwd)
    far_b = lax.ppermute(got_b[:, k:], axis, bwd)
    return chunk(0) + got_f[:, :k] + got_b[:, :k] + jnp.concatenate([far_f, far_b], axis=1)


def _all_gather4(c, axis, pos, fwd, bwd):
    m, k = c.shape
    h = k // 2
    got_f = lax.ppermute(c, axis, fwd)
    got_b = lax.ppermute(c, axis, bwd)
    far = jnp.concatenate(
        [lax.ppermute(got_f[:, :h], axis, fwd), lax.ppermute(got_b[:, h:], axis, bwd)], axis=1
    )
    out = jnp.zeros((4 * m, k), c.dtype)
    for j, blk in ((0, c), (-1, got_f), (1, got_b), (2, far)):
        out = lax.dynamic_update_slice_in_dim(out, blk, lax.rem(pos + j + 4, 4) * m, axis=0)
    return out


def _rs_small(v, axis, n, pos, fwd, bwd):
    if n == 4:
        return _reduce_scatter4(v, axis, pos, fwd, bwd)
    return _ring_reduce_scatter(v, axis, n, pos, fwd, bwd)


def _ag(c, axis, n, pos, fwd, bwd):
    if n == 4:
        return _all_gather4(c, axis, pos, fwd, bwd)
    return _ring_all_gather(c, axis, n, pos, fwd, bwd)


def _gather_cells(blk, n):
    q = lax.axis_index("cells")
    rows, w = blk.shape
    out = jnp.zeros((rows, n, w), blk.dtype)
    out = lax.dynamic_update_slice(out, blk[:, None, :], (0, q, 0))
    fwd = _perm(n, lambda i: (i + 1) % n)
    bwd = _perm(n, lambda i: (i - 1) % n)
    n_f = n // 2
    n_b = n - 1 - n_f
    cur_f = cur_b = blk
    for s in range(max(n_f, n_b)):
        if s < n_f:
            cur_f = lax.ppermute(cur_f, "cells", fwd)
            out = lax.dynamic_update_slice(out, cur_f[:, None, :], (0, lax.rem(q - s - 1 + n, n), 0))
        if s < n_b:
            cur_b = lax.ppermute(cur_b, "cells", bwd)
            out = lax.dynamic_update_slice(out, cur_b[:, None, :], (0, lax.rem(q + s + 1, n), 0))
    return out


def per_device(train_depth, train_basis, sample_basis, gram_inverse):
    runs_here, terms_here = train_basis.shape
    n_cells = lax.axis_size("cells")
    n_runs = lax.axis_size("runs")
    total_runs = train_depth.shape[0] * n_runs
    norm_scale = 1.0 / math.sqrt(total_runs)

    both = jnp.concatenate([train_basis, sample_basis], axis=1)
    both_full = _gather_cells(both, n_cells)
    train_full = both_full[:, :, :terms_here].reshape(runs_here, n_cells * terms_here)
    sample_full = both_full[:, :, terms_here:].reshape(runs_here, n_cells * terms_here)

    folded = lax.dot_general(
        train_full.astype(jnp.float32), gram_inverse, (((1,), (1,)), ((), ())),
        precision=lax.Precision.HIGHEST,
    )
    folded_hi = lax.reduce_precision(folded, exponent_bits=8, mantissa_bits=7)
    folded_lo = (folded - folded_hi).astype(jnp.bfloat16)
    folded_hi = folded_hi.astype(jnp.bfloat16)
    dims = (((0,), (0,)), ((), ()))

    def project(depth):
        return lax.dot_general(
            depth, folded_hi, dims, preferred_element_type=jnp.float32
        ) + lax.dot_general(depth, folded_lo, dims, preferred_element_type=jnp.float32)

    ny, nx, nc = _factor_runs(n_runs)
    r = lax.axis_index("runs")
    core = lax.rem(r, nc)
    xi = lax.rem(r // nc, nx)
    yi = r // (nc * nx)

    def shift_x(d):
        return lambda i: ((i // (nc * nx)) * nx + (i // nc % nx + d) % nx) * nc + i % nc

    def shift_y(d):
        return lambda i: (((i // (nc * nx)) + d) % ny * nx + i // nc % nx) * nc + i % nc

    xf, xb = _perm(n_runs, shift_x(1)), _perm(n_runs, shift_x(-1))
    yf, yb = _perm(n_runs, shift_y(1)), _perm(n_runs, shift_y(-1))

    cells_here = train_depth.shape[1]
    if nc > 1:
        core_perm = _perm(n_runs, lambda i: i - i % nc + (i % nc + 1) % nc)
        half = cells_here // nc
        other = project(lax.dynamic_slice_in_dim(train_depth, (1 - core) * half, half, axis=1))
        received = lax.ppermute(other, "runs", core_perm)
        mine = project(lax.dynamic_slice_in_dim(train_depth, core * half, half, axis=1))
        summed = received + mine
    else:
        summed = project(train_depth)
    k2 = summed.shape[1] // 2
    part_a = _ring_reduce_scatter(summed[:, :k2], "runs", nx, xi, xf, xb)
    part_a = _rs_small(part_a, "runs", ny, yi, yf, yb)
    part_b = _ring_reduce_scatter(summed[:, k2:], "runs", ny, yi, yf, yb)
    part_b = _rs_small(part_b, "runs", nx, xi, xf, xb)
    coeff_a = (part_a * norm_scale).astype(jnp.bfloat16)
    coeff_b = (part_b * norm_scale).astype(jnp.bfloat16)
    coeff_a = _ag(coeff_a, "runs", ny, yi, yf, yb)
    coeff_a = _ag(coeff_a, "runs", nx, xi, xf, xb)
    coeff_b = _ag(coeff_b, "runs", nx, xi, xf, xb)
    coeff_b = _ag(coeff_b, "runs", ny, yi, yf, yb)
    coeffs_t = jnp.concatenate([coeff_a, coeff_b], axis=1)

    def surrogate(coeffs):
        return lax.dot_general(
            sample_full, coeffs, (((1,), (1,)), ((), ())), preferred_element_type=jnp.float32
        ).astype(jnp.bfloat16)

    if nc == 1:
        return surrogate(coeffs_t)
    theirs = lax.ppermute(coeffs_t, "runs", core_perm)
    peak_depth = jnp.zeros((sample_full.shape[0], cells_here), jnp.bfloat16)
    peak_depth = lax.dynamic_update_slice_in_dim(peak_depth, surrogate(coeffs_t), core * half, axis=1)
    return lax.dynamic_update_slice_in_dim(peak_depth, surrogate(theirs), (1 - core) * half, axis=1)


def solution(mesh):
    in_specs = (P("runs", "cells"), P("runs", "cells"), P("runs", "cells"), P())
    out_specs = P("runs", "cells")
    return jax.shard_map(
        per_device, mesh=mesh, in_specs=in_specs, out_specs=out_specs, check_vma=False
    )
```

```python
import math

import jax
import jax.numpy as jnp
from jax import lax
from jax.sharding import PartitionSpec as P


def _factor_runs(n_runs):
    nc = 2 if n_runs % 2 == 0 else 1
    rest = n_runs // nc
    nx = int(math.isqrt(rest))
    while rest % nx:
        nx -= 1
    return rest // nx, nx, nc


def _perm(n, fn):
    return [(i, fn(i)) for i in range(n)]


def _ring_reduce_scatter(v, axis, n, pos, fwd, bwd):
    if isinstance(v, tuple):
        m, h = v[0].shape[0] // n, v[0].shape[1] // 2
        parts_lo = tuple(p[:, :h] for p in v)
        parts_hi = tuple(p[:, h:] for p in v)

        def piece2(srcs, idx):
            start = lax.rem(idx + 2 * n, n) * m
            total = lax.dynamic_slice_in_dim(srcs[0], start, m, axis=0)
            for p in srcs[1:]:
                total = total + lax.dynamic_slice_in_dim(p, start, m, axis=0)
            return total

        acc_f, acc_b = piece2(parts_lo, pos - 1), piece2(parts_hi, pos + 1)
        for s in range(n - 1):
            acc_f = lax.ppermute(acc_f, axis, fwd) + piece2(parts_lo, pos - s - 2)
            acc_b = lax.ppermute(acc_b, axis, bwd) + piece2(parts_hi, pos + s + 2)
        return jnp.concatenate([acc_f, acc_b], axis=1)
    if n == 1:
        return v
    m = v.shape[0] // n
    if bwd is None:
        acc = lax.dynamic_slice_in_dim(v, lax.rem(pos - 1 + n, n) * m, m, axis=0)
        for s in range(n - 1):
            acc = lax.ppermute(acc, axis, fwd) + lax.dynamic_slice_in_dim(
                v, lax.rem(pos - s - 2 + 2 * n, n) * m, m, axis=0
            )
        return acc
    h = v.shape[1] // 2
    lo, hi = v[:, :h], v[:, h:]

    def piece(src, idx):
        return lax.dynamic_slice_in_dim(src, lax.rem(idx + 2 * n, n) * m, m, axis=0)

    acc_f, acc_b = piece(lo, pos - 1), piece(hi, pos + 1)
    for s in range(n - 1):
        acc_f = lax.ppermute(acc_f, axis, fwd) + piece(lo, pos - s - 2)
        acc_b = lax.ppermute(acc_b, axis, bwd) + piece(hi, pos + s + 2)
    return jnp.concatenate([acc_f, acc_b], axis=1)


def _ring_all_gather(c, axis, n, pos, fwd, bwd):
    if n == 1:
        return c
    m, k = c.shape
    h = k // 2
    out = jnp.zeros((n * m, k), c.dtype)
    out = lax.dynamic_update_slice(out, c, (pos * m, 0))
    if bwd is None:
        cur = c
        for s in range(n - 1):
            cur = lax.ppermute(cur, axis, fwd)
            out = lax.dynamic_update_slice(out, cur, (lax.rem(pos - s - 1 + n, n) * m, 0))
        return out
    cur_f, cur_b = c[:, :h], c[:, h:]
    for s in range(n - 1):
        cur_f = lax.ppermute(cur_f, axis, fwd)
        cur_b = lax.ppermute(cur_b, axis, bwd)
        out = lax.dynamic_update_slice(out, cur_f, (lax.rem(pos - s - 1 + n, n) * m, 0))
        out = lax.dynamic_update_slice(out, cur_b, (lax.rem(pos + s + 1, n) * m, h))
    return out


def _reduce_scatter4(v, axis, pos, fwd, bwd):
    m, k = v.shape[0] // 4, v.shape[1]
    h = k // 2

    def chunk(j):
        return lax.dynamic_slice_in_dim(v, lax.rem(pos + j + 4, 4) * m, m, axis=0)

    far = chunk(2)
    got_f = lax.ppermute(jnp.concatenate([chunk(1), far[:, :h]], axis=1), axis, fwd)
    got_b = lax.ppermute(jnp.concatenate([chunk(-1), far[:, h:]], axis=1), axis, bwd)
    far_f = lax.ppermute(got_f[:, k:], axis, fwd)
    far_b = lax.ppermute(got_b[:, k:], axis, bwd)
    return chunk(0) + got_f[:, :k] + got_b[:, :k] + jnp.concatenate([far_f, far_b], axis=1)


def _all_gather4(c, axis, pos, fwd, bwd):
    m, k = c.shape
    h = k // 2
    got_f = lax.ppermute(c, axis, fwd)
    got_b = lax.ppermute(c, axis, bwd)
    far = jnp.concatenate(
        [lax.ppermute(got_f[:, :h], axis, fwd), lax.ppermute(got_b[:, h:], axis, bwd)], axis=1
    )
    out = jnp.zeros((4 * m, k), c.dtype)
    for j, blk in ((0, c), (-1, got_f), (1, got_b), (2, far)):
        out = lax.dynamic_update_slice_in_dim(out, blk, lax.rem(pos + j + 4, 4) * m, axis=0)
    return out


def _rs_small(v, axis, n, pos, fwd, bwd):
    if n == 4:
        return _reduce_scatter4(v, axis, pos, fwd, bwd)
    return _ring_reduce_scatter(v, axis, n, pos, fwd, bwd)


def _ag(c, axis, n, pos, fwd, bwd):
    if n == 4:
        return _all_gather4(c, axis, pos, fwd, bwd)
    return _ring_all_gather(c, axis, n, pos, fwd, bwd)


def _gather_cells_direct(blk, n):
    q = lax.axis_index("cells")
    rows, w = blk.shape
    out = jnp.zeros((rows, n, w), blk.dtype)
    out = lax.dynamic_update_slice(out, blk[:, None, :], (0, q, 0))
    for d in range(1, n):
        got = lax.ppermute(blk, "cells", _perm(n, lambda i, d=d: (i + d) % n))
        out = lax.dynamic_update_slice(out, got[:, None, :], (0, lax.rem(q - d + n, n), 0))
    return out


def _gather_cells(blk, n):
    q = lax.axis_index("cells")
    rows, w = blk.shape
    out = jnp.zeros((rows, n, w), blk.dtype)
    out = lax.dynamic_update_slice(out, blk[:, None, :], (0, q, 0))
    fwd = _perm(n, lambda i: (i + 1) % n)
    bwd = _perm(n, lambda i: (i - 1) % n)
    n_f = n // 2
    n_b = n - 1 - n_f
    cur_f = cur_b = blk
    for s in range(max(n_f, n_b)):
        if s < n_f:
            cur_f = lax.ppermute(cur_f, "cells", fwd)
            out = lax.dynamic_update_slice(out, cur_f[:, None, :], (0, lax.rem(q - s - 1 + n, n), 0))
        if s < n_b:
            cur_b = lax.ppermute(cur_b, "cells", bwd)
            out = lax.dynamic_update_slice(out, cur_b[:, None, :], (0, lax.rem(q + s + 1, n), 0))
    return out


def per_device(train_depth, train_basis, sample_basis, gram_inverse):
    runs_here, terms_here = train_basis.shape
    n_cells = lax.axis_size("cells")
    n_runs = lax.axis_size("runs")
    total_runs = train_depth.shape[0] * n_runs
    norm_scale = 1.0 / math.sqrt(total_runs)

    train_full = _gather_cells_direct(train_basis, n_cells).reshape(
        runs_here, n_cells * terms_here
    )
    sample_pad = jnp.pad(sample_basis, ((0, 0), (0, 128 - terms_here % 128)))
    sample_full = lax.all_gather(sample_pad, "cells", axis=1, tiled=False)[:, :, :terms_here]
    sample_full = sample_full.reshape(runs_here, n_cells * terms_here)

    folded = lax.dot_general(
        train_full.astype(jnp.float32), gram_inverse, (((1,), (1,)), ((), ())),
        precision=lax.Precision.HIGHEST,
    )
    folded_hi = lax.reduce_precision(folded, exponent_bits=8, mantissa_bits=7)
    folded_lo = (folded - folded_hi).astype(jnp.bfloat16)
    folded_hi = folded_hi.astype(jnp.bfloat16)
    dims = (((0,), (0,)), ((), ()))

    def project(depth):
        return lax.dot_general(
            depth, folded_hi, dims, preferred_element_type=jnp.float32
        ) + lax.dot_general(depth, folded_lo, dims, preferred_element_type=jnp.float32)

    ny, nx, nc = _factor_runs(n_runs)
    r = lax.axis_index("runs")
    core = lax.rem(r, nc)
    xi = lax.rem(r // nc, nx)
    yi = r // (nc * nx)

    def shift_x(d):
        return lambda i: ((i // (nc * nx)) * nx + (i // nc % nx + d) % nx) * nc + i % nc

    def shift_y(d):
        return lambda i: (((i // (nc * nx)) + d) % ny * nx + i // nc % nx) * nc + i % nc

    xf, xb = _perm(n_runs, shift_x(1)), _perm(n_runs, shift_x(-1))
    yf, yb = _perm(n_runs, shift_y(1)), _perm(n_runs, shift_y(-1))

    cells_here = train_depth.shape[1]
    if nc > 1:
        core_perm = _perm(n_runs, lambda i: i - i % nc + (i % nc + 1) % nc)
        half = cells_here // nc
        other = project(lax.dynamic_slice_in_dim(train_depth, (1 - core) * half, half, axis=1))
        received = lax.ppermute(other, "runs", core_perm)
        mine = project(lax.dynamic_slice_in_dim(train_depth, core * half, half, axis=1))
        summed = (received, mine)
    else:
        summed = (project(train_depth),)
    k2 = summed[0].shape[1] // 2
    part_a = _ring_reduce_scatter(tuple(p[:, :k2] for p in summed), "runs", nx, xi, xf, xb)
    part_a = _rs_small(part_a, "runs", ny, yi, yf, yb)
    part_b = _ring_reduce_scatter(tuple(p[:, k2:] for p in summed), "runs", ny, yi, yf, yb)
    part_b = _rs_small(part_b, "runs", nx, xi, xf, xb)
    coeff_a = (part_a * norm_scale).astype(jnp.bfloat16)
    coeff_b = (part_b * norm_scale).astype(jnp.bfloat16)
    coeff_a = _ag(coeff_a, "runs", ny, yi, yf, yb)
    coeff_a = _ag(coeff_a, "runs", nx, xi, xf, xb)
    coeff_b = _ag(coeff_b, "runs", nx, xi, xf, xb)
    coeff_b = _ag(coeff_b, "runs", ny, yi, yf, yb)
    coeffs_t = jnp.concatenate([coeff_a, coeff_b], axis=1)

    def surrogate(coeffs):
        return lax.dot_general(
            sample_full, coeffs, (((1,), (1,)), ((), ())), preferred_element_type=jnp.float32
        ).astype(jnp.bfloat16)

    if nc == 1:
        return surrogate(coeffs_t)
    theirs = lax.ppermute(coeffs_t, "runs", core_perm)
    peak_depth = jnp.zeros((sample_full.shape[0], cells_here), jnp.bfloat16)
    peak_depth = lax.dynamic_update_slice_in_dim(peak_depth, surrogate(coeffs_t), core * half, axis=1)
    return lax.dynamic_update_slice_in_dim(peak_depth, surrogate(theirs), (1 - core) * half, axis=1)


def solution(mesh):
    in_specs = (P("runs", "cells"), P("runs", "cells"), P("runs", "cells"), P())
    out_specs = P("runs", "cells")
    return jax.shard_map(
        per_device, mesh=mesh, in_specs=in_specs, out_specs=out_specs, check_vma=False
    )
```

```python
import math

import jax
import jax.numpy as jnp
from jax import lax
from jax.sharding import PartitionSpec as P


def _factor_runs(n_runs):
    nc = 2 if n_runs % 2 == 0 else 1
    rest = n_runs // nc
    nx = int(math.isqrt(rest))
    while rest % nx:
        nx -= 1
    return rest // nx, nx, nc


def _perm(n, fn):
    return [(i, fn(i)) for i in range(n)]


def _ring_reduce_scatter(v, axis, n, pos, fwd, bwd):
    if isinstance(v, tuple):
        m, h = v[0].shape[0] // n, v[0].shape[1] // 2
        parts_lo = tuple(p[:, :h] for p in v)
        parts_hi = tuple(p[:, h:] for p in v)

        def piece2(srcs, idx):
            start = lax.rem(idx + 2 * n, n) * m
            total = lax.dynamic_slice_in_dim(srcs[0], start, m, axis=0)
            for p in srcs[1:]:
                total = total + lax.dynamic_slice_in_dim(p, start, m, axis=0)
            return total

        acc_f, acc_b = piece2(parts_lo, pos - 1), piece2(parts_hi, pos + 1)
        for s in range(n - 1):
            acc_f = lax.ppermute(acc_f, axis, fwd) + piece2(parts_lo, pos - s - 2)
            acc_b = lax.ppermute(acc_b, axis, bwd) + piece2(parts_hi, pos + s + 2)
        return jnp.concatenate([acc_f, acc_b], axis=1)
    if n == 1:
        return v
    m = v.shape[0] // n
    if bwd is None:
        acc = lax.dynamic_slice_in_dim(v, lax.rem(pos - 1 + n, n) * m, m, axis=0)
        for s in range(n - 1):
            acc = lax.ppermute(acc, axis, fwd) + lax.dynamic_slice_in_dim(
                v, lax.rem(pos - s - 2 + 2 * n, n) * m, m, axis=0
            )
        return acc
    h = v.shape[1] // 2
    lo, hi = v[:, :h], v[:, h:]

    def piece(src, idx):
        return lax.dynamic_slice_in_dim(src, lax.rem(idx + 2 * n, n) * m, m, axis=0)

    acc_f, acc_b = piece(lo, pos - 1), piece(hi, pos + 1)
    for s in range(n - 1):
        acc_f = lax.ppermute(acc_f, axis, fwd) + piece(lo, pos - s - 2)
        acc_b = lax.ppermute(acc_b, axis, bwd) + piece(hi, pos + s + 2)
    return jnp.concatenate([acc_f, acc_b], axis=1)


def _ring_all_gather(c, axis, n, pos, fwd, bwd):
    if n == 1:
        return c
    m, k = c.shape
    h = k // 2
    out = jnp.zeros((n * m, k), c.dtype)
    out = lax.dynamic_update_slice(out, c, (pos * m, 0))
    if bwd is None:
        cur = c
        for s in range(n - 1):
            cur = lax.ppermute(cur, axis, fwd)
            out = lax.dynamic_update_slice(out, cur, (lax.rem(pos - s - 1 + n, n) * m, 0))
        return out
    cur_f, cur_b = c[:, :h], c[:, h:]
    for s in range(n - 1):
        cur_f = lax.ppermute(cur_f, axis, fwd)
        cur_b = lax.ppermute(cur_b, axis, bwd)
        out = lax.dynamic_update_slice(out, cur_f, (lax.rem(pos - s - 1 + n, n) * m, 0))
        out = lax.dynamic_update_slice(out, cur_b, (lax.rem(pos + s + 1, n) * m, h))
    return out


def _reduce_scatter4(v, axis, pos, fwd, bwd):
    m, k = v.shape[0] // 4, v.shape[1]
    h = k // 2

    def chunk(j):
        return lax.dynamic_slice_in_dim(v, lax.rem(pos + j + 4, 4) * m, m, axis=0)

    far = chunk(2)
    got_f = lax.ppermute(jnp.concatenate([chunk(1), far[:, :h]], axis=1), axis, fwd)
    got_b = lax.ppermute(jnp.concatenate([chunk(-1), far[:, h:]], axis=1), axis, bwd)
    far_f = lax.ppermute(got_f[:, k:], axis, fwd)
    far_b = lax.ppermute(got_b[:, k:], axis, bwd)
    return chunk(0) + got_f[:, :k] + got_b[:, :k] + jnp.concatenate([far_f, far_b], axis=1)


def _all_gather4(c, axis, pos, fwd, bwd):
    m, k = c.shape
    h = k // 2
    got_f = lax.ppermute(c, axis, fwd)
    got_b = lax.ppermute(c, axis, bwd)
    far = jnp.concatenate(
        [lax.ppermute(got_f[:, :h], axis, fwd), lax.ppermute(got_b[:, h:], axis, bwd)], axis=1
    )
    out = jnp.zeros((4 * m, k), c.dtype)
    for j, blk in ((0, c), (-1, got_f), (1, got_b), (2, far)):
        out = lax.dynamic_update_slice_in_dim(out, blk, lax.rem(pos + j + 4, 4) * m, axis=0)
    return out


def _rs_small(v, axis, n, pos, fwd, bwd):
    if n == 4:
        return _reduce_scatter4(v, axis, pos, fwd, bwd)
    return _ring_reduce_scatter(v, axis, n, pos, fwd, bwd)


def _ag(c, axis, n, pos, fwd, bwd):
    if n == 4:
        return _all_gather4(c, axis, pos, fwd, bwd)
    return _ring_all_gather(c, axis, n, pos, fwd, bwd)


def _gather_cells_direct(blk, n):
    q = lax.axis_index("cells")
    rows, w = blk.shape
    out = jnp.zeros((rows, n, w), blk.dtype)
    out = lax.dynamic_update_slice(out, blk[:, None, :], (0, q, 0))
    for d in range(1, n):
        got = lax.ppermute(blk, "cells", _perm(n, lambda i, d=d: (i + d) % n))
        out = lax.dynamic_update_slice(out, got[:, None, :], (0, lax.rem(q - d + n, n), 0))
    return out


def _gather_cells(blk, n):
    q = lax.axis_index("cells")
    rows, w = blk.shape
    out = jnp.zeros((rows, n, w), blk.dtype)
    out = lax.dynamic_update_slice(out, blk[:, None, :], (0, q, 0))
    fwd = _perm(n, lambda i: (i + 1) % n)
    bwd = _perm(n, lambda i: (i - 1) % n)
    n_f = n // 2
    n_b = n - 1 - n_f
    cur_f = cur_b = blk
    for s in range(max(n_f, n_b)):
        if s < n_f:
            cur_f = lax.ppermute(cur_f, "cells", fwd)
            out = lax.dynamic_update_slice(out, cur_f[:, None, :], (0, lax.rem(q - s - 1 + n, n), 0))
        if s < n_b:
            cur_b = lax.ppermute(cur_b, "cells", bwd)
            out = lax.dynamic_update_slice(out, cur_b[:, None, :], (0, lax.rem(q + s + 1, n), 0))
    return out


def per_device(train_depth, train_basis, sample_basis, gram_inverse):
    runs_here, terms_here = train_basis.shape
    n_cells = lax.axis_size("cells")
    n_runs = lax.axis_size("runs")
    total_runs = train_depth.shape[0] * n_runs
    norm_scale = 1.0 / math.sqrt(total_runs)

    train_full = _gather_cells_direct(train_basis, n_cells).reshape(
        runs_here, n_cells * terms_here
    )
    sample_in, train_full = lax.optimization_barrier((sample_basis, train_full))
    sample_full = _gather_cells_direct(sample_in, n_cells).reshape(
        runs_here, n_cells * terms_here
    )

    folded = lax.dot_general(
        train_full.astype(jnp.float32), gram_inverse, (((1,), (1,)), ((), ())),
        precision=lax.Precision.HIGHEST,
    )
    folded_hi = lax.reduce_precision(folded, exponent_bits=8, mantissa_bits=7)
    folded_lo = (folded - folded_hi).astype(jnp.bfloat16)
    folded_hi = folded_hi.astype(jnp.bfloat16)
    dims = (((0,), (0,)), ((), ()))

    def project(depth):
        return lax.dot_general(
            depth, folded_hi, dims, preferred_element_type=jnp.float32
        ) + lax.dot_general(depth, folded_lo, dims, preferred_element_type=jnp.float32)

    ny, nx, nc = _factor_runs(n_runs)
    r = lax.axis_index("runs")
    core = lax.rem(r, nc)
    xi = lax.rem(r // nc, nx)
    yi = r // (nc * nx)

    def shift_x(d):
        return lambda i: ((i // (nc * nx)) * nx + (i // nc % nx + d) % nx) * nc + i % nc

    def shift_y(d):
        return lambda i: (((i // (nc * nx)) + d) % ny * nx + i // nc % nx) * nc + i % nc

    xf, xb = _perm(n_runs, shift_x(1)), _perm(n_runs, shift_x(-1))
    yf, yb = _perm(n_runs, shift_y(1)), _perm(n_runs, shift_y(-1))

    cells_here = train_depth.shape[1]
    if nc > 1:
        core_perm = _perm(n_runs, lambda i: i - i % nc + (i % nc + 1) % nc)
        half = cells_here // nc
        other = project(lax.dynamic_slice_in_dim(train_depth, (1 - core) * half, half, axis=1))
        received = lax.ppermute(other, "runs", core_perm)
        received, sample_full = lax.optimization_barrier((received, sample_full))
        mine = project(lax.dynamic_slice_in_dim(train_depth, core * half, half, axis=1))
        summed = (received, mine)
    else:
        summed = (project(train_depth),)
    k2 = summed[0].shape[1] // 2
    part_a = _ring_reduce_scatter(tuple(p[:, :k2] for p in summed), "runs", nx, xi, xf, xb)
    part_a = _rs_small(part_a, "runs", ny, yi, yf, yb)
    part_b = _ring_reduce_scatter(tuple(p[:, k2:] for p in summed), "runs", ny, yi, yf, yb)
    part_b = _rs_small(part_b, "runs", nx, xi, xf, xb)
    coeff_a = (part_a * norm_scale).astype(jnp.bfloat16)
    coeff_b = (part_b * norm_scale).astype(jnp.bfloat16)
    coeff_a = _ag(coeff_a, "runs", ny, yi, yf, yb)
    coeff_a = _ag(coeff_a, "runs", nx, xi, xf, xb)
    coeff_b = _ag(coeff_b, "runs", nx, xi, xf, xb)
    coeff_b = _ag(coeff_b, "runs", ny, yi, yf, yb)
    coeffs_t = jnp.concatenate([coeff_a, coeff_b], axis=1)

    def surrogate(coeffs):
        return lax.dot_general(
            sample_full, coeffs, (((1,), (1,)), ((), ())), preferred_element_type=jnp.float32
        ).astype(jnp.bfloat16)

    if nc == 1:
        return surrogate(coeffs_t)
    theirs = lax.ppermute(coeffs_t, "runs", core_perm)
    peak_depth = jnp.zeros((sample_full.shape[0], cells_here), jnp.bfloat16)
    peak_depth = lax.dynamic_update_slice_in_dim(peak_depth, surrogate(coeffs_t), core * half, axis=1)
    return lax.dynamic_update_slice_in_dim(peak_depth, surrogate(theirs), (1 - core) * half, axis=1)


def solution(mesh):
    in_specs = (P("runs", "cells"), P("runs", "cells"), P("runs", "cells"), P())
    out_specs = P("runs", "cells")
    return jax.shard_map(
        per_device, mesh=mesh, in_specs=in_specs, out_specs=out_specs, check_vma=False
    )
```

```python
import math

import jax
import jax.numpy as jnp
from jax import lax
from jax.sharding import PartitionSpec as P


def _factor_runs(n_runs):
    nc = 2 if n_runs % 2 == 0 else 1
    rest = n_runs // nc
    nx = int(math.isqrt(rest))
    while rest % nx:
        nx -= 1
    return rest // nx, nx, nc


def _perm(n, fn):
    return [(i, fn(i)) for i in range(n)]


def _ring_reduce_scatter(v, axis, n, pos, fwd, bwd):
    if n == 1:
        return v
    m = v.shape[0] // n
    if bwd is None:
        acc = lax.dynamic_slice_in_dim(v, lax.rem(pos - 1 + n, n) * m, m, axis=0)
        for s in range(n - 1):
            acc = lax.ppermute(acc, axis, fwd) + lax.dynamic_slice_in_dim(
                v, lax.rem(pos - s - 2 + 2 * n, n) * m, m, axis=0
            )
        return acc
    h = v.shape[1] // 2
    lo, hi = v[:, :h], v[:, h:]

    def piece(src, idx):
        return lax.dynamic_slice_in_dim(src, lax.rem(idx + 2 * n, n) * m, m, axis=0)

    acc_f, acc_b = piece(lo, pos - 1), piece(hi, pos + 1)
    for s in range(n - 1):
        acc_f = lax.ppermute(acc_f, axis, fwd) + piece(lo, pos - s - 2)
        acc_b = lax.ppermute(acc_b, axis, bwd) + piece(hi, pos + s + 2)
    return jnp.concatenate([acc_f, acc_b], axis=1)


def _ring_all_gather(c, axis, n, pos, fwd, bwd):
    if n == 1:
        return c
    m, k = c.shape
    h = k // 2
    out = jnp.zeros((n * m, k), c.dtype)
    out = lax.dynamic_update_slice(out, c, (pos * m, 0))
    if bwd is None:
        cur = c
        for s in range(n - 1):
            cur = lax.ppermute(cur, axis, fwd)
            out = lax.dynamic_update_slice(out, cur, (lax.rem(pos - s - 1 + n, n) * m, 0))
        return out
    cur_f, cur_b = c[:, :h], c[:, h:]
    for s in range(n - 1):
        cur_f = lax.ppermute(cur_f, axis, fwd)
        cur_b = lax.ppermute(cur_b, axis, bwd)
        out = lax.dynamic_update_slice(out, cur_f, (lax.rem(pos - s - 1 + n, n) * m, 0))
        out = lax.dynamic_update_slice(out, cur_b, (lax.rem(pos + s + 1, n) * m, h))
    return out


def _reduce_scatter4(v, axis, pos, fwd, bwd):
    m, k = v.shape[0] // 4, v.shape[1]
    h = k // 2

    def chunk(j):
        return lax.dynamic_slice_in_dim(v, lax.rem(pos + j + 4, 4) * m, m, axis=0)

    far = chunk(2)
    got_f = lax.ppermute(jnp.concatenate([chunk(1), far[:, :h]], axis=1), axis, fwd)
    got_b = lax.ppermute(jnp.concatenate([chunk(-1), far[:, h:]], axis=1), axis, bwd)
    far_f = lax.ppermute(got_f[:, k:], axis, fwd)
    far_b = lax.ppermute(got_b[:, k:], axis, bwd)
    return chunk(0) + got_f[:, :k] + got_b[:, :k] + jnp.concatenate([far_f, far_b], axis=1)


def _all_gather4(c, axis, pos, fwd, bwd):
    m, k = c.shape
    h = k // 2
    got_f = lax.ppermute(c, axis, fwd)
    got_b = lax.ppermute(c, axis, bwd)
    far = jnp.concatenate(
        [lax.ppermute(got_f[:, :h], axis, fwd), lax.ppermute(got_b[:, h:], axis, bwd)], axis=1
    )
    out = jnp.zeros((4 * m, k), c.dtype)
    for j, blk in ((0, c), (-1, got_f), (1, got_b), (2, far)):
        out = lax.dynamic_update_slice_in_dim(out, blk, lax.rem(pos + j + 4, 4) * m, axis=0)
    return out


def _rs_small(v, axis, n, pos, fwd, bwd):
    if n == 4:
        return _reduce_scatter4(v, axis, pos, fwd, bwd)
    return _ring_reduce_scatter(v, axis, n, pos, fwd, bwd)


def _ag(c, axis, n, pos, fwd, bwd):
    if n == 4:
        return _all_gather4(c, axis, pos, fwd, bwd)
    return _ring_all_gather(c, axis, n, pos, fwd, bwd)


def _gather_cells(blk, n):
    q = lax.axis_index("cells")
    rows, w = blk.shape
    out = jnp.zeros((rows, n, w), blk.dtype)
    out = lax.dynamic_update_slice(out, blk[:, None, :], (0, q, 0))
    fwd = _perm(n, lambda i: (i + 1) % n)
    bwd = _perm(n, lambda i: (i - 1) % n)
    n_f = n // 2
    n_b = n - 1 - n_f
    cur_f = cur_b = blk
    for s in range(max(n_f, n_b)):
        if s < n_f:
            cur_f = lax.ppermute(cur_f, "cells", fwd)
            out = lax.dynamic_update_slice(out, cur_f[:, None, :], (0, lax.rem(q - s - 1 + n, n), 0))
        if s < n_b:
            cur_b = lax.ppermute(cur_b, "cells", bwd)
            out = lax.dynamic_update_slice(out, cur_b[:, None, :], (0, lax.rem(q + s + 1, n), 0))
    return out


def per_device(train_depth, train_basis, sample_basis, gram_inverse):
    runs_here, terms_here = train_basis.shape
    n_cells = lax.axis_size("cells")
    n_runs = lax.axis_size("runs")
    total_runs = train_depth.shape[0] * n_runs
    norm_scale = 1.0 / math.sqrt(total_runs)

    both = jnp.concatenate([train_basis, sample_basis], axis=1)
    both_full = _gather_cells(both, n_cells)
    train_full = both_full[:, :, :terms_here].reshape(runs_here, n_cells * terms_here)
    sample_full = both_full[:, :, terms_here:].reshape(runs_here, n_cells * terms_here)

    folded = lax.dot_general(
        train_full.astype(jnp.float32), gram_inverse, (((1,), (1,)), ((), ())),
        precision=lax.Precision.HIGHEST,
    )
    folded_hi = lax.reduce_precision(folded, exponent_bits=8, mantissa_bits=7)
    folded_lo = (folded - folded_hi).astype(jnp.bfloat16)
    folded_hi = folded_hi.astype(jnp.bfloat16)
    dims = (((0,), (0,)), ((), ()))

    def project(depth):
        return lax.dot_general(
            depth, folded_hi, dims, preferred_element_type=jnp.float32
        ) + lax.dot_general(depth, folded_lo, dims, preferred_element_type=jnp.float32)

    ny, nx, nc = _factor_runs(n_runs)
    r = lax.axis_index("runs")
    core = lax.rem(r, nc)
    xi = lax.rem(r // nc, nx)
    yi = r // (nc * nx)

    def shift_x(d):
        return lambda i: ((i // (nc * nx)) * nx + (i // nc % nx + d) % nx) * nc + i % nc

    def shift_y(d):
        return lambda i: (((i // (nc * nx)) + d) % ny * nx + i // nc % nx) * nc + i % nc

    xf, xb = _perm(n_runs, shift_x(1)), _perm(n_runs, shift_x(-1))
    yf, yb = _perm(n_runs, shift_y(1)), _perm(n_runs, shift_y(-1))

    cells_here = train_depth.shape[1]
    if nc > 1:
        core_perm = _perm(n_runs, lambda i: i - i % nc + (i % nc + 1) % nc)
        half = cells_here // nc
        other = project(lax.dynamic_slice_in_dim(train_depth, (1 - core) * half, half, axis=1))
        received = lax.ppermute(other, "runs", core_perm)
        mine = project(lax.dynamic_slice_in_dim(train_depth, core * half, half, axis=1))
        summed = received + mine
    else:
        summed = project(train_depth)
    k2 = summed.shape[1] // 2
    part_a = _rs_small(summed[:, :k2], "runs", nx, xi, xf, xb)
    part_a = _rs_small(part_a, "runs", ny, yi, yf, yb)
    part_b = _rs_small(summed[:, k2:], "runs", ny, yi, yf, yb)
    part_b = _rs_small(part_b, "runs", nx, xi, xf, xb)
    coeff_a = (part_a * norm_scale).astype(jnp.bfloat16)
    coeff_b = (part_b * norm_scale).astype(jnp.bfloat16)
    coeff_a = _ag(coeff_a, "runs", ny, yi, yf, yb)
    coeff_a = _ag(coeff_a, "runs", nx, xi, xf, xb)
    coeff_b = _ag(coeff_b, "runs", nx, xi, xf, xb)
    coeff_b = _ag(coeff_b, "runs", ny, yi, yf, yb)
    coeffs_t = jnp.concatenate([coeff_a, coeff_b], axis=1)

    def surrogate(coeffs):
        return lax.dot_general(
            sample_full, coeffs, (((1,), (1,)), ((), ())), preferred_element_type=jnp.float32
        ).astype(jnp.bfloat16)

    if nc == 1:
        return surrogate(coeffs_t)
    theirs = lax.ppermute(coeffs_t, "runs", core_perm)
    peak_depth = jnp.zeros((sample_full.shape[0], cells_here), jnp.bfloat16)
    peak_depth = lax.dynamic_update_slice_in_dim(peak_depth, surrogate(coeffs_t), core * half, axis=1)
    return lax.dynamic_update_slice_in_dim(peak_depth, surrogate(theirs), (1 - core) * half, axis=1)


def solution(mesh):
    in_specs = (P("runs", "cells"), P("runs", "cells"), P("runs", "cells"), P())
    out_specs = P("runs", "cells")
    return jax.shard_map(
        per_device, mesh=mesh, in_specs=in_specs, out_specs=out_specs, check_vma=False
    )
```

```python
import math

import jax
import jax.numpy as jnp
from jax import lax
from jax.sharding import PartitionSpec as P


def _factor_runs(n_runs):
    nc = 2 if n_runs % 2 == 0 else 1
    rest = n_runs // nc
    nx = int(math.isqrt(rest))
    while rest % nx:
        nx -= 1
    return rest // nx, nx, nc


def _perm(n, fn):
    return [(i, fn(i)) for i in range(n)]


def _ring_reduce_scatter(v, axis, n, pos, fwd, bwd):
    if n == 1:
        return v
    m = v.shape[0] // n
    if bwd is None:
        acc = lax.dynamic_slice_in_dim(v, lax.rem(pos - 1 + n, n) * m, m, axis=0)
        for s in range(n - 1):
            acc = lax.ppermute(acc, axis, fwd) + lax.dynamic_slice_in_dim(
                v, lax.rem(pos - s - 2 + 2 * n, n) * m, m, axis=0
            )
        return acc
    h = v.shape[1] // 2
    lo, hi = v[:, :h], v[:, h:]

    def piece(src, idx):
        return lax.dynamic_slice_in_dim(src, lax.rem(idx + 2 * n, n) * m, m, axis=0)

    acc_f, acc_b = piece(lo, pos - 1), piece(hi, pos + 1)
    for s in range(n - 1):
        acc_f = lax.ppermute(acc_f, axis, fwd) + piece(lo, pos - s - 2)
        acc_b = lax.ppermute(acc_b, axis, bwd) + piece(hi, pos + s + 2)
    return jnp.concatenate([acc_f, acc_b], axis=1)


def _ring_all_gather(c, axis, n, pos, fwd, bwd):
    if n == 1:
        return c
    m, k = c.shape
    h = k // 2
    out = jnp.zeros((n * m, k), c.dtype)
    out = lax.dynamic_update_slice(out, c, (pos * m, 0))
    if bwd is None:
        cur = c
        for s in range(n - 1):
            cur = lax.ppermute(cur, axis, fwd)
            out = lax.dynamic_update_slice(out, cur, (lax.rem(pos - s - 1 + n, n) * m, 0))
        return out
    cur_f, cur_b = c[:, :h], c[:, h:]
    for s in range(n - 1):
        cur_f = lax.ppermute(cur_f, axis, fwd)
        cur_b = lax.ppermute(cur_b, axis, bwd)
        out = lax.dynamic_update_slice(out, cur_f, (lax.rem(pos - s - 1 + n, n) * m, 0))
        out = lax.dynamic_update_slice(out, cur_b, (lax.rem(pos + s + 1, n) * m, h))
    return out


def _reduce_scatter4(v, axis, pos, fwd, bwd):
    m, k = v.shape[0] // 4, v.shape[1]
    h = k // 2

    def chunk(j):
        return lax.dynamic_slice_in_dim(v, lax.rem(pos + j + 4, 4) * m, m, axis=0)

    far = chunk(2)
    got_f = lax.ppermute(jnp.concatenate([chunk(1), far[:, :h]], axis=1), axis, fwd)
    got_b = lax.ppermute(jnp.concatenate([chunk(-1), far[:, h:]], axis=1), axis, bwd)
    far_f = lax.ppermute(got_f[:, k:], axis, fwd)
    far_b = lax.ppermute(got_b[:, k:], axis, bwd)
    return chunk(0) + got_f[:, :k] + got_b[:, :k] + jnp.concatenate([far_f, far_b], axis=1)


def _all_gather4(c, axis, pos, fwd, bwd):
    m, k = c.shape
    h = k // 2
    got_f = lax.ppermute(c, axis, fwd)
    got_b = lax.ppermute(c, axis, bwd)
    far = jnp.concatenate(
        [lax.ppermute(got_f[:, :h], axis, fwd), lax.ppermute(got_b[:, h:], axis, bwd)], axis=1
    )
    rel = jnp.concatenate([c, got_b, far, got_f], axis=0)
    return lax.dynamic_slice_in_dim(jnp.concatenate([rel, rel], axis=0), (4 - pos) * m, 4 * m, axis=0)


def _rs_small(v, axis, n, pos, fwd, bwd):
    if n == 4:
        return _reduce_scatter4(v, axis, pos, fwd, bwd)
    return _ring_reduce_scatter(v, axis, n, pos, fwd, bwd)


def _ag(c, axis, n, pos, fwd, bwd):
    if n == 4:
        return _all_gather4(c, axis, pos, fwd, bwd)
    return _ring_all_gather(c, axis, n, pos, fwd, bwd)


def _gather_cells(blk, n):
    q = lax.axis_index("cells")
    fwd = _perm(n, lambda i: (i + 1) % n)
    bwd = _perm(n, lambda i: (i - 1) % n)
    n_f = n // 2
    n_b = n - 1 - n_f
    got = {0: blk}
    cur_f = cur_b = blk
    for s in range(max(n_f, n_b)):
        if s < n_f:
            cur_f = lax.ppermute(cur_f, "cells", fwd)
            got[n - s - 1] = cur_f
        if s < n_b:
            cur_b = lax.ppermute(cur_b, "cells", bwd)
            got[s + 1] = cur_b
    rel = jnp.stack([got[d] for d in range(n)], axis=1)
    both = jnp.concatenate([rel, rel], axis=1)
    return lax.dynamic_slice_in_dim(both, n - q, n, axis=1)


def per_device(train_depth, train_basis, sample_basis, gram_inverse):
    runs_here, terms_here = train_basis.shape
    n_cells = lax.axis_size("cells")
    n_runs = lax.axis_size("runs")
    total_runs = train_depth.shape[0] * n_runs
    norm_scale = 1.0 / math.sqrt(total_runs)

    both = jnp.concatenate([train_basis, sample_basis], axis=1)
    both_full = _gather_cells(both, n_cells)
    train_full = both_full[:, :, :terms_here].reshape(runs_here, n_cells * terms_here)
    sample_full = both_full[:, :, terms_here:].reshape(runs_here, n_cells * terms_here)

    folded = lax.dot_general(
        train_full.astype(jnp.float32), gram_inverse, (((1,), (1,)), ((), ())),
        precision=lax.Precision.HIGHEST,
    )
    folded_hi = lax.reduce_precision(folded, exponent_bits=8, mantissa_bits=7)
    folded_lo = (folded - folded_hi).astype(jnp.bfloat16)
    folded_hi = folded_hi.astype(jnp.bfloat16)
    dims = (((0,), (0,)), ((), ()))

    def project(depth):
        return lax.dot_general(
            depth, folded_hi, dims, preferred_element_type=jnp.float32
        ) + lax.dot_general(depth, folded_lo, dims, preferred_element_type=jnp.float32)

    ny, nx, nc = _factor_runs(n_runs)
    r = lax.axis_index("runs")
    core = lax.rem(r, nc)
    xi = lax.rem(r // nc, nx)
    yi = r // (nc * nx)

    def shift_x(d):
        return lambda i: ((i // (nc * nx)) * nx + (i // nc % nx + d) % nx) * nc + i % nc

    def shift_y(d):
        return lambda i: (((i // (nc * nx)) + d) % ny * nx + i // nc % nx) * nc + i % nc

    xf, xb = _perm(n_runs, shift_x(1)), _perm(n_runs, shift_x(-1))
    yf, yb = _perm(n_runs, shift_y(1)), _perm(n_runs, shift_y(-1))

    cells_here = train_depth.shape[1]
    if nc > 1:
        core_perm = _perm(n_runs, lambda i: i - i % nc + (i % nc + 1) % nc)
        half = cells_here // nc
        other = project(lax.dynamic_slice_in_dim(train_depth, (1 - core) * half, half, axis=1))
        received = lax.ppermute(other, "runs", core_perm)
        mine = project(lax.dynamic_slice_in_dim(train_depth, core * half, half, axis=1))
        summed = received + mine
    else:
        summed = project(train_depth)
    k2 = summed.shape[1] // 2
    part_a = _ring_reduce_scatter(summed[:, :k2], "runs", nx, xi, xf, xb)
    part_a = _rs_small(part_a, "runs", ny, yi, yf, yb)
    part_b = _ring_reduce_scatter(summed[:, k2:], "runs", ny, yi, yf, yb)
    part_b = _rs_small(part_b, "runs", nx, xi, xf, xb)
    coeff_a = (part_a * norm_scale).astype(jnp.bfloat16)
    coeff_b = (part_b * norm_scale).astype(jnp.bfloat16)
    coeff_a = _ag(coeff_a, "runs", ny, yi, yf, yb)
    coeff_a = _ag(coeff_a, "runs", nx, xi, xf, xb)
    coeff_b = _ag(coeff_b, "runs", nx, xi, xf, xb)
    coeff_b = _ag(coeff_b, "runs", ny, yi, yf, yb)
    coeffs_t = jnp.concatenate([coeff_a, coeff_b], axis=1)

    def surrogate(coeffs):
        return lax.dot_general(
            sample_full, coeffs, (((1,), (1,)), ((), ())), preferred_element_type=jnp.float32
        ).astype(jnp.bfloat16)

    if nc == 1:
        return surrogate(coeffs_t)
    theirs = lax.ppermute(coeffs_t, "runs", core_perm)
    peak_depth = jnp.zeros((sample_full.shape[0], cells_here), jnp.bfloat16)
    peak_depth = lax.dynamic_update_slice_in_dim(peak_depth, surrogate(coeffs_t), core * half, axis=1)
    return lax.dynamic_update_slice_in_dim(peak_depth, surrogate(theirs), (1 - core) * half, axis=1)


def solution(mesh):
    in_specs = (P("runs", "cells"), P("runs", "cells"), P("runs", "cells"), P())
    out_specs = P("runs", "cells")
    return jax.shard_map(
        per_device, mesh=mesh, in_specs=in_specs, out_specs=out_specs, check_vma=False
    )
```

```python
import math

import jax
import jax.numpy as jnp
from jax import lax
from jax.sharding import PartitionSpec as P


def _factor_runs(n_runs):
    nc = 2 if n_runs % 2 == 0 else 1
    rest = n_runs // nc
    nx = int(math.isqrt(rest))
    while rest % nx:
        nx -= 1
    return rest // nx, nx, nc


def _perm(n, fn):
    return [(i, fn(i)) for i in range(n)]


def _ring_reduce_scatter(v, axis, n, pos, fwd, bwd):
    if n == 1:
        return v
    m = v.shape[0] // n
    if bwd is None:
        acc = lax.dynamic_slice_in_dim(v, lax.rem(pos - 1 + n, n) * m, m, axis=0)
        for s in range(n - 1):
            acc = lax.ppermute(acc, axis, fwd) + lax.dynamic_slice_in_dim(
                v, lax.rem(pos - s - 2 + 2 * n, n) * m, m, axis=0
            )
        return acc
    h = v.shape[1] // 2
    lo, hi = v[:, :h], v[:, h:]

    def piece(src, idx):
        return lax.dynamic_slice_in_dim(src, lax.rem(idx + 2 * n, n) * m, m, axis=0)

    acc_f, acc_b = piece(lo, pos - 1), piece(hi, pos + 1)
    for s in range(n - 1):
        acc_f = lax.ppermute(acc_f, axis, fwd) + piece(lo, pos - s - 2)
        acc_b = lax.ppermute(acc_b, axis, bwd) + piece(hi, pos + s + 2)
    return jnp.concatenate([acc_f, acc_b], axis=1)


def _ring_all_gather(c, axis, n, pos, fwd, bwd):
    if n == 1:
        return c
    m, k = c.shape
    h = k // 2
    out = jnp.zeros((n * m, k), c.dtype)
    out = lax.dynamic_update_slice(out, c, (pos * m, 0))
    if bwd is None:
        cur = c
        for s in range(n - 1):
            cur = lax.ppermute(cur, axis, fwd)
            out = lax.dynamic_update_slice(out, cur, (lax.rem(pos - s - 1 + n, n) * m, 0))
        return out
    cur_f, cur_b = c[:, :h], c[:, h:]
    for s in range(n - 1):
        cur_f = lax.ppermute(cur_f, axis, fwd)
        cur_b = lax.ppermute(cur_b, axis, bwd)
        out = lax.dynamic_update_slice(out, cur_f, (lax.rem(pos - s - 1 + n, n) * m, 0))
        out = lax.dynamic_update_slice(out, cur_b, (lax.rem(pos + s + 1, n) * m, h))
    return out


def _reduce_scatter4(v, axis, pos, fwd, bwd):
    m, k = v.shape[0] // 4, v.shape[1]
    h = k // 2

    def chunk(j):
        return lax.dynamic_slice_in_dim(v, lax.rem(pos + j + 4, 4) * m, m, axis=0)

    far = chunk(2)
    got_f = lax.ppermute(jnp.concatenate([chunk(1), far[:, :h]], axis=1), axis, fwd)
    got_b = lax.ppermute(jnp.concatenate([chunk(-1), far[:, h:]], axis=1), axis, bwd)
    far_f = lax.ppermute(got_f[:, k:], axis, fwd)
    far_b = lax.ppermute(got_b[:, k:], axis, bwd)
    return chunk(0) + got_f[:, :k] + got_b[:, :k] + jnp.concatenate([far_f, far_b], axis=1)


def _all_gather4(c, axis, pos, fwd, bwd):
    m, k = c.shape
    h = k // 2
    got_f = lax.ppermute(c, axis, fwd)
    got_b = lax.ppermute(c, axis, bwd)
    far = jnp.concatenate(
        [lax.ppermute(got_f[:, :h], axis, fwd), lax.ppermute(got_b[:, h:], axis, bwd)], axis=1
    )
    out = jnp.zeros((4 * m, k), c.dtype)
    for j, blk in ((0, c), (-1, got_f), (1, got_b), (2, far)):
        out = lax.dynamic_update_slice_in_dim(out, blk, lax.rem(pos + j + 4, 4) * m, axis=0)
    return out


def _rs_small(v, axis, n, pos, fwd, bwd):
    if n == 4:
        return _reduce_scatter4(v, axis, pos, fwd, bwd)
    return _ring_reduce_scatter(v, axis, n, pos, fwd, bwd)


def _ag(c, axis, n, pos, fwd, bwd):
    if n == 4:
        return _all_gather4(c, axis, pos, fwd, bwd)
    return _ring_all_gather(c, axis, n, pos, fwd, bwd)


def _gather_cells(blk, n):
    q = lax.axis_index("cells")
    rows, w = blk.shape
    out = jnp.zeros((rows, n, w), blk.dtype)
    out = lax.dynamic_update_slice(out, blk[:, None, :], (0, q, 0))
    fwd = _perm(n, lambda i: (i + 1) % n)
    bwd = _perm(n, lambda i: (i - 1) % n)
    n_f = n // 2
    n_b = n - 1 - n_f
    cur_f = cur_b = blk
    for s in range(max(n_f, n_b)):
        if s < n_f:
            cur_f = lax.ppermute(cur_f, "cells", fwd)
            out = lax.dynamic_update_slice(out, cur_f[:, None, :], (0, lax.rem(q - s - 1 + n, n), 0))
        if s < n_b:
            cur_b = lax.ppermute(cur_b, "cells", bwd)
            out = lax.dynamic_update_slice(out, cur_b[:, None, :], (0, lax.rem(q + s + 1, n), 0))
    return out


def per_device(train_depth, train_basis, sample_basis, gram_inverse):
    runs_here, terms_here = train_basis.shape
    n_cells = lax.axis_size("cells")
    n_runs = lax.axis_size("runs")
    total_runs = train_depth.shape[0] * n_runs
    norm_scale = 1.0 / math.sqrt(total_runs)

    both = jnp.concatenate([train_basis, sample_basis], axis=1)
    both_full = _gather_cells(both, n_cells)
    train_full = both_full[:, :, :terms_here].reshape(runs_here, n_cells * terms_here)
    sample_full = both_full[:, :, terms_here:].reshape(runs_here, n_cells * terms_here)

    folded = lax.dot_general(
        train_full.astype(jnp.float32), gram_inverse, (((1,), (1,)), ((), ())),
        precision=lax.Precision.HIGHEST,
    )
    folded_hi = lax.reduce_precision(folded, exponent_bits=8, mantissa_bits=7)
    folded_lo = (folded - folded_hi).astype(jnp.bfloat16)
    folded_hi = folded_hi.astype(jnp.bfloat16)
    dims = (((0,), (0,)), ((), ()))

    folded_both = jnp.concatenate([folded_hi, folded_lo], axis=0)

    def project(depth):
        return lax.dot_general(
            jnp.concatenate([depth, depth], axis=0), folded_both, dims,
            preferred_element_type=jnp.float32,
        )

    ny, nx, nc = _factor_runs(n_runs)
    r = lax.axis_index("runs")
    core = lax.rem(r, nc)
    xi = lax.rem(r // nc, nx)
    yi = r // (nc * nx)

    def shift_x(d):
        return lambda i: ((i // (nc * nx)) * nx + (i // nc % nx + d) % nx) * nc + i % nc

    def shift_y(d):
        return lambda i: (((i // (nc * nx)) + d) % ny * nx + i // nc % nx) * nc + i % nc

    xf, xb = _perm(n_runs, shift_x(1)), _perm(n_runs, shift_x(-1))
    yf, yb = _perm(n_runs, shift_y(1)), _perm(n_runs, shift_y(-1))

    cells_here = train_depth.shape[1]
    if nc > 1:
        core_perm = _perm(n_runs, lambda i: i - i % nc + (i % nc + 1) % nc)
        half = cells_here // nc
        other = project(lax.dynamic_slice_in_dim(train_depth, (1 - core) * half, half, axis=1))
        received = lax.ppermute(other, "runs", core_perm)
        mine = project(lax.dynamic_slice_in_dim(train_depth, core * half, half, axis=1))
        summed = received + mine
    else:
        summed = project(train_depth)
    k2 = summed.shape[1] // 2
    part_a = _ring_reduce_scatter(summed[:, :k2], "runs", nx, xi, xf, xb)
    part_a = _rs_small(part_a, "runs", ny, yi, yf, yb)
    part_b = _ring_reduce_scatter(summed[:, k2:], "runs", ny, yi, yf, yb)
    part_b = _rs_small(part_b, "runs", nx, xi, xf, xb)
    coeff_a = (part_a * norm_scale).astype(jnp.bfloat16)
    coeff_b = (part_b * norm_scale).astype(jnp.bfloat16)
    coeff_a = _ag(coeff_a, "runs", ny, yi, yf, yb)
    coeff_a = _ag(coeff_a, "runs", nx, xi, xf, xb)
    coeff_b = _ag(coeff_b, "runs", nx, xi, xf, xb)
    coeff_b = _ag(coeff_b, "runs", ny, yi, yf, yb)
    coeffs_t = jnp.concatenate([coeff_a, coeff_b], axis=1)

    def surrogate(coeffs):
        return lax.dot_general(
            sample_full, coeffs, (((1,), (1,)), ((), ())), preferred_element_type=jnp.float32
        ).astype(jnp.bfloat16)

    if nc == 1:
        return surrogate(coeffs_t)
    theirs = lax.ppermute(coeffs_t, "runs", core_perm)
    peak_depth = jnp.zeros((sample_full.shape[0], cells_here), jnp.bfloat16)
    peak_depth = lax.dynamic_update_slice_in_dim(peak_depth, surrogate(coeffs_t), core * half, axis=1)
    return lax.dynamic_update_slice_in_dim(peak_depth, surrogate(theirs), (1 - core) * half, axis=1)


def solution(mesh):
    in_specs = (P("runs", "cells"), P("runs", "cells"), P("runs", "cells"), P())
    out_specs = P("runs", "cells")
    return jax.shard_map(
        per_device, mesh=mesh, in_specs=in_specs, out_specs=out_specs, check_vma=False
    )
```

```python
import math

import jax
import jax.numpy as jnp
from jax import lax
from jax.sharding import PartitionSpec as P


def _factor_runs(n_runs):
    nc = 2 if n_runs % 2 == 0 else 1
    rest = n_runs // nc
    nx = int(math.isqrt(rest))
    while rest % nx:
        nx -= 1
    return rest // nx, nx, nc


def _perm(n, fn):
    return [(i, fn(i)) for i in range(n)]


def _ring_reduce_scatter(v, axis, n, pos, fwd, bwd):
    if n == 1:
        return v
    m = v.shape[0] // n
    if bwd is None:
        acc = lax.dynamic_slice_in_dim(v, lax.rem(pos - 1 + n, n) * m, m, axis=0)
        for s in range(n - 1):
            acc = lax.ppermute(acc, axis, fwd) + lax.dynamic_slice_in_dim(
                v, lax.rem(pos - s - 2 + 2 * n, n) * m, m, axis=0
            )
        return acc
    h = v.shape[1] // 2
    lo, hi = v[:, :h], v[:, h:]

    def piece(src, idx):
        return lax.dynamic_slice_in_dim(src, lax.rem(idx + 2 * n, n) * m, m, axis=0)

    acc_f, acc_b = piece(lo, pos - 1), piece(hi, pos + 1)
    for s in range(n - 1):
        acc_f = lax.ppermute(acc_f, axis, fwd) + piece(lo, pos - s - 2)
        acc_b = lax.ppermute(acc_b, axis, bwd) + piece(hi, pos + s + 2)
    return jnp.concatenate([acc_f, acc_b], axis=1)


def _ring_all_gather(c, axis, n, pos, fwd, bwd):
    if n == 1:
        return c
    m, k = c.shape
    h = k // 2
    out = jnp.zeros((n * m, k), c.dtype)
    out = lax.dynamic_update_slice(out, c, (pos * m, 0))
    if bwd is None:
        cur = c
        for s in range(n - 1):
            cur = lax.ppermute(cur, axis, fwd)
            out = lax.dynamic_update_slice(out, cur, (lax.rem(pos - s - 1 + n, n) * m, 0))
        return out
    cur_f, cur_b = c[:, :h], c[:, h:]
    for s in range(n - 1):
        cur_f = lax.ppermute(cur_f, axis, fwd)
        cur_b = lax.ppermute(cur_b, axis, bwd)
        out = lax.dynamic_update_slice(out, cur_f, (lax.rem(pos - s - 1 + n, n) * m, 0))
        out = lax.dynamic_update_slice(out, cur_b, (lax.rem(pos + s + 1, n) * m, h))
    return out


def _reduce_scatter4(v, axis, pos, fwd, bwd):
    m, k = v.shape[0] // 4, v.shape[1]
    h = k // 2

    def chunk(j):
        return lax.dynamic_slice_in_dim(v, lax.rem(pos + j + 4, 4) * m, m, axis=0)

    far = chunk(2)
    got_f = lax.ppermute(jnp.concatenate([chunk(1), far[:, :h]], axis=1), axis, fwd)
    got_b = lax.ppermute(jnp.concatenate([chunk(-1), far[:, h:]], axis=1), axis, bwd)
    far_f = lax.ppermute(got_f[:, k:], axis, fwd)
    far_b = lax.ppermute(got_b[:, k:], axis, bwd)
    return chunk(0) + got_f[:, :k] + got_b[:, :k] + jnp.concatenate([far_f, far_b], axis=1)


def _all_gather4(c, axis, pos, fwd, bwd):
    m, k = c.shape
    h = k // 2
    got_f = lax.ppermute(c, axis, fwd)
    got_b = lax.ppermute(c, axis, bwd)
    far = jnp.concatenate(
        [lax.ppermute(got_f[:, :h], axis, fwd), lax.ppermute(got_b[:, h:], axis, bwd)], axis=1
    )
    out = jnp.zeros((4 * m, k), c.dtype)
    for j, blk in ((0, c), (-1, got_f), (1, got_b), (2, far)):
        out = lax.dynamic_update_slice_in_dim(out, blk, lax.rem(pos + j + 4, 4) * m, axis=0)
    return out


def _rs_small(v, axis, n, pos, fwd, bwd):
    if n == 4:
        return _reduce_scatter4(v, axis, pos, fwd, bwd)
    return _ring_reduce_scatter(v, axis, n, pos, fwd, bwd)


def _ag(c, axis, n, pos, fwd, bwd):
    if n == 4:
        return _all_gather4(c, axis, pos, fwd, bwd)
    return _ring_all_gather(c, axis, n, pos, fwd, bwd)


def _gather_cells(blk, n):
    q = lax.axis_index("cells")
    rows, w = blk.shape
    out = jnp.zeros((rows, n, w), blk.dtype)
    out = lax.dynamic_update_slice(out, blk[:, None, :], (0, q, 0))
    fwd = _perm(n, lambda i: (i + 1) % n)
    bwd = _perm(n, lambda i: (i - 1) % n)
    n_f = n // 2
    n_b = n - 1 - n_f
    cur_f = cur_b = blk
    for s in range(max(n_f, n_b)):
        if s < n_f:
            cur_f = lax.ppermute(cur_f, "cells", fwd)
            out = lax.dynamic_update_slice(out, cur_f[:, None, :], (0, lax.rem(q - s - 1 + n, n), 0))
        if s < n_b:
            cur_b = lax.ppermute(cur_b, "cells", bwd)
            out = lax.dynamic_update_slice(out, cur_b[:, None, :], (0, lax.rem(q + s + 1, n), 0))
    return out


def per_device(train_depth, train_basis, sample_basis, gram_inverse):
    runs_here, terms_here = train_basis.shape
    n_cells = lax.axis_size("cells")
    n_runs = lax.axis_size("runs")
    total_runs = train_depth.shape[0] * n_runs
    norm_scale = 1.0 / math.sqrt(total_runs)

    both = jnp.concatenate([train_basis, sample_basis], axis=1)
    both_full = _gather_cells(both, n_cells)
    train_full = both_full[:, :, :terms_here].reshape(runs_here, n_cells * terms_here)
    sample_full = both_full[:, :, terms_here:].reshape(runs_here, n_cells * terms_here)

    folded = lax.dot_general(
        train_full.astype(jnp.float32), gram_inverse, (((1,), (1,)), ((), ())),
        precision=lax.Precision.HIGHEST,
    )
    folded_hi = lax.reduce_precision(folded, exponent_bits=8, mantissa_bits=7)
    folded_lo = (folded - folded_hi).astype(jnp.bfloat16)
    folded_hi = folded_hi.astype(jnp.bfloat16)
    dims = (((0,), (0,)), ((), ()))

    folded_both = jnp.concatenate([folded_hi, folded_lo], axis=0)

    def project(depth):
        return lax.dot_general(
            jnp.concatenate([depth, depth], axis=0), folded_both, dims,
            preferred_element_type=jnp.float32,
        )

    ny, nx, nc = _factor_runs(n_runs)
    r = lax.axis_index("runs")
    core = lax.rem(r, nc)
    xi = lax.rem(r // nc, nx)
    yi = r // (nc * nx)

    def shift_x(d):
        return lambda i: ((i // (nc * nx)) * nx + (i // nc % nx + d) % nx) * nc + i % nc

    def shift_y(d):
        return lambda i: (((i // (nc * nx)) + d) % ny * nx + i // nc % nx) * nc + i % nc

    xf, xb = _perm(n_runs, shift_x(1)), _perm(n_runs, shift_x(-1))
    yf, yb = _perm(n_runs, shift_y(1)), _perm(n_runs, shift_y(-1))

    cells_here = train_depth.shape[1]
    if nc > 1:
        core_perm = _perm(n_runs, lambda i: i - i % nc + (i % nc + 1) % nc)
        half = cells_here // nc
        other = project(lax.dynamic_slice_in_dim(train_depth, (1 - core) * half, half, axis=1))
        received = lax.ppermute(other, "runs", core_perm)
        mine = project(lax.dynamic_slice_in_dim(train_depth, core * half, half, axis=1))
        summed = received + mine
    else:
        summed = project(train_depth)
    k2 = summed.shape[1] // 2
    part_a = _ring_reduce_scatter(summed[:, :k2], "runs", nx, xi, xf, xb)
    part_a = _rs_small(part_a, "runs", ny, yi, yf, yb)
    part_b = _ring_reduce_scatter(summed[:, k2:], "runs", ny, yi, yf, yb)
    part_b = _rs_small(part_b, "runs", nx, xi, xf, xb)
    coeff_a = (part_a * norm_scale).astype(jnp.bfloat16)
    coeff_b = (part_b * norm_scale).astype(jnp.bfloat16)
    coeff_a = _ring_all_gather(coeff_a, "runs", ny, yi, yf, None)
    coeff_a = _ag(coeff_a, "runs", nx, xi, xf, xb)
    coeff_b = _ring_all_gather(coeff_b, "runs", nx, xi, xf, None)
    coeff_b = _ag(coeff_b, "runs", ny, yi, yf, yb)
    coeffs_t = jnp.concatenate([coeff_a, coeff_b], axis=1)

    def surrogate(coeffs):
        return lax.dot_general(
            sample_full, coeffs, (((1,), (1,)), ((), ())), preferred_element_type=jnp.float32
        ).astype(jnp.bfloat16)

    if nc == 1:
        return surrogate(coeffs_t)
    theirs = lax.ppermute(coeffs_t, "runs", core_perm)
    peak_depth = jnp.zeros((sample_full.shape[0], cells_here), jnp.bfloat16)
    peak_depth = lax.dynamic_update_slice_in_dim(peak_depth, surrogate(coeffs_t), core * half, axis=1)
    return lax.dynamic_update_slice_in_dim(peak_depth, surrogate(theirs), (1 - core) * half, axis=1)


def solution(mesh):
    in_specs = (P("runs", "cells"), P("runs", "cells"), P("runs", "cells"), P())
    out_specs = P("runs", "cells")
    return jax.shard_map(
        per_device, mesh=mesh, in_specs=in_specs, out_specs=out_specs, check_vma=False
    )
```
